256 devices in a mesh: seg: 4 (over x_lo, core), utt: 64 (over y, x_hi, z).
Axes of the slice: x: 4 (x_hi: 2, x_lo: 2; x = x_hi * 2 + x_lo), y: 4, z: 8, core: 2. Of those that a mesh axis runs over, the one named last changes fastest.
Arguments:
- audio_waves: float32 [64, 4096], P('utt', 'seg'), may hold values from -6 to 6
- lengths: int32 [64], P('utt'), may hold values from 1024 to 4096
- target_ids: int32 [64, 32], P('utt', 'seg'), may hold values from 0 to 255
- input_weight: float32 [128], replicated, may hold values from -4 to 4
- conv_weight: bfloat16 [10, 256, 512], replicated, may hold values from -0.375 to 0.375
- res_weight: bfloat16 [9, 256, 128], replicated, may hold values from -0.375 to 0.375
- skip_weight: bfloat16 [2560, 1024], replicated, may hold values from -0.375 to 0.375
Outputs:
- gram: float32 [1024, 1024], P(('seg', 'utt'))
- cross: float32 [1024, 256], P(('seg', 'utt'))
The draws below stay inside these ranges and needn't reach their ends.
All inputs are finite; a program needn't handle non-finite values.
Results may differ from the reference program's by a relative error of at most 0.0023.
Values may be sent and summed in bfloat16 or wider, within the bound.
No kernel may reach another device: no remote copies, remote signals or barrier semaphores. Data moves between devices by JAX's collectives and lax.ppermute only.
A program may use at most 64 MiB of HBM per device.

```python
import jax
import jax.numpy as jnp
from jax import lax

D_RES = 128
D_GATE = 256
D_SKIP = 1024
CLASSES = 256
LAYERS = 10
SEG_LEN = 1024
FRAME = 128
UTTS = 64
SAMPLES = 4096


def with_ends(values, own_key, smallest, largest):
    longest = values.shape.index(max(values.shape))
    spots = []
    for shift in (0, 1):
        where = [jax.random.randint(jax.random.fold_in(own_key, axis), (), 0, length) for axis, length in enumerate(values.shape)]
        where[longest] = (where[longest] + shift) % values.shape[longest]
        spots.append(tuple(where))
    return values.at[spots[0]].set(smallest).at[spots[1]].set(largest)


def block_levels(key, dims, split, smallest, top_value):
    level = 1.0
    for position, parts in split:
        heights = jax.random.uniform(jax.random.fold_in(jax.random.fold_in(key, 6), position), (parts,), jnp.float32, smallest / len(split), top_value / len(split))
        level = level * jnp.repeat(jnp.exp(heights), dims[position] // parts).reshape((-1,) + (1,) * (len(dims) - 1 - position))
    return level


def bell_draw(key, shape, scale, bound, pieces=(), kind=jnp.bfloat16):
    gain = block_levels(key, shape, pieces, -0.22, 0.18) if pieces else 1.0
    array = jax.random.normal(key, shape, jnp.float32) * scale * gain
    return jnp.minimum(jnp.maximum(array, -bound), bound).astype(kind)


def setup_inputs(seed: int = 0) -> dict:
    seeds = jax.random.split(jax.random.key(seed), 8)
    return {
        "audio_waves": bell_draw(seeds[0], (UTTS, SAMPLES), 1.0, 6.0, ((0, 64), (1, 4)), jnp.float32),
        "lengths": with_ends(jax.random.randint(seeds[1], (UTTS,), SEG_LEN, SAMPLES + 1), jax.random.fold_in(seeds[1], 1), SEG_LEN, SAMPLES).astype(jnp.int32),
        "target_ids": with_ends(jax.random.randint(seeds[2], (UTTS, SAMPLES // FRAME), 0, CLASSES), jax.random.fold_in(seeds[2], 1), 0, CLASSES - 1).astype(jnp.int32),
        "input_weight": bell_draw(seeds[3], (D_RES,), 1.0, 4.0, (), jnp.float32),
        "conv_weight": bell_draw(seeds[4], (LAYERS, 2 * D_RES, 2 * D_GATE), (2 * D_RES) ** -0.5, 0.375),
        "res_weight": bell_draw(seeds[5], (LAYERS - 1, D_GATE, D_RES), D_GATE ** -0.5, 0.375),
        "skip_weight": bell_draw(seeds[6], (LAYERS * D_GATE, D_SKIP), D_GATE ** -0.5, 0.375),
    }


HALF_ROOT = 0.7071067811865476


def encode(wave_row, input_weight, conv_weight, res_weight, skip_weight):
    hidden = (wave_row[:, None] * input_weight[None, :]).astype(jnp.bfloat16)
    gated_list = []
    for layer_num in range(LAYERS):
        dilation = 2 ** layer_num
        delayed = jnp.concatenate([jnp.zeros((dilation, D_RES), jnp.bfloat16), hidden[:-dilation]], 0)
        paired = jnp.concatenate([delayed, hidden], 1)
        preact = jnp.dot(paired, conv_weight[layer_num], preferred_element_type=jnp.float32)
        gated = (jnp.tanh(preact[:, :D_GATE]) * jax.nn.sigmoid(preact[:, D_GATE:])).astype(jnp.bfloat16)
        gated_list.append(gated)
        if layer_num < LAYERS - 1:
            residual_term = jnp.dot(gated, res_weight[layer_num], preferred_element_type=jnp.float32)
            hidden = ((hidden.astype(jnp.float32) + residual_term) * HALF_ROOT).astype(jnp.bfloat16)
    stacked = jnp.concatenate(gated_list, 1)
    skip_sum = jnp.dot(stacked, skip_weight, preferred_element_type=jnp.float32)
    return jnp.maximum(skip_sum, 0.0).astype(jnp.bfloat16)


def reference(audio_waves, lengths, target_ids, input_weight, conv_weight, res_weight, skip_weight):
    def one_utterance(carry, items):
        wave_row, length_one, ids_row = items
        features = encode(wave_row, input_weight, conv_weight, res_weight, skip_weight)
        valid = jnp.arange(SAMPLES, dtype=jnp.int32) < length_one
        masked = jnp.where(valid[:, None], features, jnp.zeros_like(features))
        frame_ids = jnp.repeat(ids_row, FRAME)
        onehot = (frame_ids[:, None] == jnp.arange(CLASSES, dtype=jnp.int32)[None, :]).astype(jnp.bfloat16)
        paired = jnp.concatenate([masked, onehot], 1)
        term = lax.dot_general(masked, paired, (((0,), (0,)), ((), ())), preferred_element_type=jnp.float32)
        return carry + term, None

    start_sum = jnp.zeros((D_SKIP, D_SKIP + CLASSES), jnp.float32)
    totals, _ = lax.scan(one_utterance, start_sum, (audio_waves, lengths, target_ids))
    count = jnp.sum(lengths.astype(jnp.float32))
    gram = totals[:, :D_SKIP] / count
    cross = totals[:, D_SKIP:] * (CLASSES / count)
    return gram, cross
```

```python
import jax
import jax.numpy as jnp
from jax import lax
from jax.sharding import PartitionSpec as P

CLASSES = 256
FRAME = 128


HALF_ROOT = 0.7071067811865476


def shifted(value, axis, by):
    length = lax.axis_size(axis)
    pairs = [(i, i + by) for i in range(length) if 0 <= i + by < length]
    return lax.ppermute(value, axis, pairs)


def round_up(value, step):
    return -(-value // step) * step


def layer_math(delayed, current, conv_one, res_one):
    channels = current.shape[1]
    paired = jnp.concatenate([delayed, current], 1)
    preact = jnp.dot(paired, conv_one, preferred_element_type=jnp.float32)
    gate_width = preact.shape[1] // 2
    gated = (jnp.tanh(preact[:, :gate_width]) * jax.nn.sigmoid(preact[:, gate_width:])).astype(
        jnp.bfloat16
    )
    following = None
    if res_one is not None:
        residual_term = jnp.dot(gated, res_one, preferred_element_type=jnp.float32)
        following = ((current.astype(jnp.float32) + residual_term) * HALF_ROOT).astype(
            jnp.bfloat16
        )
    return gated, following


def per_device(
    audio_waves, lengths, target_ids, input_weight, conv_weight, res_weight, skip_weight
):
    batch_rows, seg_len = audio_waves.shape
    layer_total = conv_weight.shape[0]
    reach = 2**layer_total - 1
    earlier = shifted(audio_waves, "seg", 1)
    window = round_up(seg_len + reach, 16)
    extended = jnp.concatenate([earlier, audio_waves], 1)[0, 2 * seg_len - window :]
    hidden = (extended[:, None] * input_weight[None, :]).astype(jnp.bfloat16)
    gated_list = []
    for layer_num in range(layer_total):
        dilation = 2**layer_num
        later_reach = 2**layer_total - 2 ** (layer_num + 1)
        in_len = hidden.shape[0]
        out_len = min(in_len, round_up(seg_len + later_reach, 16))
        if in_len - dilation >= out_len:
            delayed = hidden[in_len - out_len - dilation : in_len - dilation]
        else:
            delayed = jnp.concatenate(
                [jnp.zeros((dilation, hidden.shape[1]), hidden.dtype), hidden[: in_len - dilation]],
                0,
            )
        current = hidden[in_len - out_len :]
        res_one = res_weight[layer_num] if layer_num < layer_total - 1 else None
        gated, hidden = layer_math(delayed, current, conv_weight[layer_num], res_one)
        gated_list.append(gated[out_len - seg_len :])
    stacked = jnp.concatenate(gated_list, 1)
    skip_sum = jnp.dot(stacked, skip_weight, preferred_element_type=jnp.float32)
    features = jnp.maximum(skip_sum, 0.0).astype(jnp.bfloat16)
    skip_width = features.shape[1]
    position = lax.axis_index("seg") * seg_len + jnp.arange(seg_len, dtype=jnp.int32)
    valid = (position[None, :] < lengths[:, None]).reshape(batch_rows * seg_len)
    masked = jnp.where(valid[:, None], features, jnp.zeros_like(features))
    frame_ids = jnp.repeat(target_ids, FRAME, axis=1).reshape(batch_rows * seg_len)
    onehot = (frame_ids[:, None] == jnp.arange(CLASSES, dtype=jnp.int32)[None, :]).astype(
        jnp.bfloat16
    )
    paired = jnp.concatenate([masked, onehot], 1)
    valid_total = lax.psum(jnp.sum(lengths), "utt").astype(jnp.float32)
    partial = lax.dot_general(
        masked, paired, (((0,), (0,)), ((), ())), preferred_element_type=jnp.float32
    )
    owners = lax.axis_size("seg") * lax.axis_size("utt")
    row_count = partial.shape[0] // owners
    width = partial.shape[1]
    slab = partial.reshape(owners, 8, row_count * width // 8)
    owned = lax.psum_scatter(slab, ("seg", "utt"), scatter_dimension=0, tiled=True)
    owned_rows = owned.reshape(row_count, width)
    gram_rows = owned_rows[:, :skip_width] / valid_total
    cross_rows = owned_rows[:, skip_width:] * (CLASSES / valid_total)
    return (gram_rows, cross_rows)


def solution(mesh):
    in_specs = (P("utt", "seg"), P("utt"), P("utt", "seg"), P(), P(), P(), P())
    out_specs = (P(("seg", "utt"), None), P(("seg", "utt"), None))
    return jax.shard_map(
        per_device, mesh=mesh, in_specs=in_specs, out_specs=out_specs, check_vma=False
    )
```

```python
import jax
import jax.numpy as jnp
from jax import lax
from jax.sharding import Mesh, PartitionSpec as P

CLASSES = 256
FRAME = 128


HALF_ROOT = 0.7071067811865476


SEG = ("xl", "core")
UTT = ("y", "xh", "z")
FINE = SEG + UTT
STAGES = ("core", "z", "y", "xh", "xl")


def fine_sizes(seg_size, utt_size):
    z = 8 if utt_size % 8 == 0 else utt_size
    xh = 2 if (utt_size // z) % 2 == 0 else 1
    return {"xl": seg_size // 2, "core": 2, "y": utt_size // (z * xh), "xh": xh, "z": z}


def shifted(value, axis, by):
    length = 1
    for name in axis:
        length *= lax.axis_size(name)
    pairs = [(i, i + by) for i in range(length) if 0 <= i + by < length]
    return lax.ppermute(value, axis, pairs)


def round_up(value, step):
    return -(-value // step) * step


def layer_math(delayed, current, conv_one, res_one):
    channels = current.shape[1]
    paired = jnp.concatenate([delayed, current], 1)
    preact = jnp.dot(paired, conv_one, preferred_element_type=jnp.float32)
    gate_width = preact.shape[1] // 2
    gated = (jnp.tanh(preact[:, :gate_width]) * jax.nn.sigmoid(preact[:, gate_width:])).astype(
        jnp.bfloat16
    )
    following = None
    if res_one is not None:
        residual_term = jnp.dot(gated, res_one, preferred_element_type=jnp.float32)
        following = ((current.astype(jnp.float32) + residual_term) * HALF_ROOT).astype(
            jnp.bfloat16
        )
    return gated, following


def per_device(
    audio_waves, lengths, target_ids, input_weight, conv_weight, res_weight, skip_weight
):
    batch_rows, seg_len = audio_waves.shape
    layer_total = conv_weight.shape[0]
    reach = 2**layer_total - 1
    earlier = shifted(audio_waves, SEG, 1)
    window = round_up(seg_len + reach, 16)
    extended = jnp.concatenate([earlier, audio_waves], 1)[0, 2 * seg_len - window :]
    hidden = (extended[:, None] * input_weight[None, :]).astype(jnp.bfloat16)
    gated_list = []
    for layer_num in range(layer_total):
        dilation = 2**layer_num
        later_reach = 2**layer_total - 2 ** (layer_num + 1)
        in_len = hidden.shape[0]
        out_len = min(in_len, round_up(seg_len + later_reach, 16))
        if in_len - dilation >= out_len:
            delayed = hidden[in_len - out_len - dilation : in_len - dilation]
        else:
            delayed = jnp.concatenate(
                [jnp.zeros((dilation, hidden.shape[1]), hidden.dtype), hidden[: in_len - dilation]],
                0,
            )
        current = hidden[in_len - out_len :]
        res_one = res_weight[layer_num] if layer_num < layer_total - 1 else None
        gated, hidden = layer_math(delayed, current, conv_weight[layer_num], res_one)
        gated_list.append(gated[out_len - seg_len :])
    stacked = jnp.concatenate(gated_list, 1)
    skip_sum = jnp.dot(stacked, skip_weight, preferred_element_type=jnp.float32)
    features = jnp.maximum(skip_sum, 0.0).astype(jnp.bfloat16)
    skip_width = features.shape[1]
    position = lax.axis_index(SEG) * seg_len + jnp.arange(seg_len, dtype=jnp.int32)
    valid = (position[None, :] < lengths[:, None]).reshape(batch_rows * seg_len)
    masked = jnp.where(valid[:, None], features, jnp.zeros_like(features))
    frame_ids = jnp.repeat(target_ids, FRAME, axis=1).reshape(batch_rows * seg_len)
    onehot = (frame_ids[:, None] == jnp.arange(CLASSES, dtype=jnp.int32)[None, :]).astype(
        jnp.bfloat16
    )
    paired = jnp.concatenate([masked, onehot], 1)
    valid_total = lax.psum(lengths.astype(jnp.float32), UTT)[0]
    partial = lax.dot_general(
        masked, paired, (((0,), (0,)), ((), ())), preferred_element_type=jnp.float32
    )
    sizes = {name: lax.axis_size(name) for name in FINE}
    owners = 1
    for name in FINE:
        owners *= sizes[name]
    row_count = partial.shape[0] // owners
    width = partial.shape[1]
    blocks = partial.reshape(tuple(sizes[n] for n in FINE) + (row_count, width))
    order = tuple(FINE.index(n) for n in STAGES) + (len(FINE), len(FINE) + 1)
    slab = blocks.transpose(order).reshape(
        tuple(sizes[n] for n in STAGES) + (8, row_count * width // 8)
    )
    for stage, name in enumerate(STAGES):
        slab = lax.psum_scatter(slab, name, scatter_dimension=stage, tiled=True)
    owned_rows = slab.reshape(row_count, width)
    gram_rows = owned_rows[:, :skip_width] / valid_total
    cross_rows = owned_rows[:, skip_width:] * (CLASSES / valid_total)
    return (gram_rows, cross_rows)


def solution(mesh):
    sizes = fine_sizes(mesh.shape["seg"], mesh.shape["utt"])
    fine = Mesh(mesh.devices.reshape(tuple(sizes[n] for n in FINE)), FINE)
    in_specs = (P(UTT, SEG), P(UTT), P(UTT, SEG), P(), P(), P(), P())
    out_specs = (P(FINE, None), P(FINE, None))
    return jax.shard_map(
        per_device, mesh=fine, in_specs=in_specs, out_specs=out_specs, check_vma=False
    )
```

```python
import jax
import jax.numpy as jnp
from jax import lax
from jax.sharding import Mesh, PartitionSpec as P

CLASSES = 256
FRAME = 128


HALF_ROOT = 0.7071067811865476


SEG = ("xl", "core")
UTT = ("y", "xh", "z")
FINE = SEG + UTT
GROUPS = (("core",), ("z",), ("y", "xh", "xl"))


def linear(index, names, sizes):
    value = 0
    for name in names:
        value = value * sizes[name] + index[name]
    return value


def owner_pairs(sizes):
    import itertools

    pairs = []
    for digits in itertools.product(*(range(sizes[n]) for n in FINE)):
        index = dict(zip(FINE, digits))
        block = 0
        for group in GROUPS:
            size = 1
            for name in group:
                size *= sizes[name]
            block = block * size + linear(index, group, sizes)
        pairs.append((linear(index, FINE, sizes), block))
    return pairs


def fine_sizes(seg_size, utt_size):
    z = 8 if utt_size % 8 == 0 else utt_size
    xh = 2 if (utt_size // z) % 2 == 0 else 1
    return {"xl": seg_size // 2, "core": 2, "y": utt_size // (z * xh), "xh": xh, "z": z}


def shifted(value, axis, by):
    length = 1
    for name in axis:
        length *= lax.axis_size(name)
    pairs = [(i, i + by) for i in range(length) if 0 <= i + by < length]
    return lax.ppermute(value, axis, pairs)


def round_up(value, step):
    return -(-value // step) * step


def layer_math(delayed, current, conv_one, res_one):
    channels = current.shape[1]
    paired = jnp.concatenate([delayed, current], 1)
    preact = jnp.dot(paired, conv_one, preferred_element_type=jnp.float32)
    gate_width = preact.shape[1] // 2
    gated = (jnp.tanh(preact[:, :gate_width]) * jax.nn.sigmoid(preact[:, gate_width:])).astype(
        jnp.bfloat16
    )
    following = None
    if res_one is not None:
        residual_term = jnp.dot(gated, res_one, preferred_element_type=jnp.float32)
        following = ((current.astype(jnp.float32) + residual_term) * HALF_ROOT).astype(
            jnp.bfloat16
        )
    return gated, following


def per_device(
    audio_waves, lengths, target_ids, input_weight, conv_weight, res_weight, skip_weight
):
    batch_rows, seg_len = audio_waves.shape
    layer_total = conv_weight.shape[0]
    reach = 2**layer_total - 1
    earlier = shifted(audio_waves, SEG, 1)
    window = round_up(seg_len + reach, 16)
    extended = jnp.concatenate([earlier, audio_waves], 1)[0, 2 * seg_len - window :]
    hidden = (extended[:, None] * input_weight[None, :]).astype(jnp.bfloat16)
    gated_list = []
    for layer_num in range(layer_total):
        dilation = 2**layer_num
        later_reach = 2**layer_total - 2 ** (layer_num + 1)
        in_len = hidden.shape[0]
        out_len = min(in_len, round_up(seg_len + later_reach, 16))
        if in_len - dilation >= out_len:
            delayed = hidden[in_len - out_len - dilation : in_len - dilation]
        else:
            delayed = jnp.concatenate(
                [jnp.zeros((dilation, hidden.shape[1]), hidden.dtype), hidden[: in_len - dilation]],
                0,
            )
        current = hidden[in_len - out_len :]
        res_one = res_weight[layer_num] if layer_num < layer_total - 1 else None
        gated, hidden = layer_math(delayed, current, conv_weight[layer_num], res_one)
        gated_list.append(gated[out_len - seg_len :])
    stacked = jnp.concatenate(gated_list, 1)
    skip_sum = jnp.dot(stacked, skip_weight, preferred_element_type=jnp.float32)
    features = jnp.maximum(skip_sum, 0.0).astype(jnp.bfloat16)
    skip_width = features.shape[1]
    position = lax.axis_index(SEG) * seg_len + jnp.arange(seg_len, dtype=jnp.int32)
    valid = (position[None, :] < lengths[:, None]).reshape(batch_rows * seg_len)
    masked = jnp.where(valid[:, None], features, jnp.zeros_like(features))
    frame_ids = jnp.repeat(target_ids, FRAME, axis=1).reshape(batch_rows * seg_len)
    onehot = (frame_ids[:, None] == jnp.arange(CLASSES, dtype=jnp.int32)[None, :]).astype(
        jnp.bfloat16
    )
    paired = jnp.concatenate([masked, onehot], 1)
    partial = lax.dot_general(
        masked, paired, (((0,), (0,)), ((), ())), preferred_element_type=jnp.float32
    )
    sizes = {name: lax.axis_size(name) for name in FINE}
    owners = 1
    for name in FINE:
        owners *= sizes[name]
    row_count = partial.shape[0] // owners
    width = partial.shape[1]
    group_sizes = []
    for group in GROUPS:
        size = 1
        for name in group:
            size *= sizes[name]
        group_sizes.append(size)
    chunk = (8, row_count * width // 8)
    slab = partial.reshape(tuple(group_sizes) + chunk)
    local_count = jnp.sum(valid.astype(jnp.float32))
    count_block = jnp.broadcast_to(local_count, tuple(group_sizes[:-1]) + (1,) + chunk)
    slab = jnp.concatenate([slab, count_block], len(GROUPS) - 1)
    for stage, group in enumerate(GROUPS[:-1]):
        slab = lax.psum_scatter(slab, group, scatter_dimension=stage, tiled=True)
    last = GROUPS[-1]
    slab = lax.psum(slab, last)
    flat = slab.reshape((group_sizes[-1] + 1,) + chunk)
    valid_total = flat[group_sizes[-1], 0, 0]
    mine = lax.dynamic_index_in_dim(flat, lax.axis_index(last), 0, keepdims=True)
    slab = lax.ppermute(mine, FINE, owner_pairs(sizes))
    owned_rows = slab.reshape(row_count, width)
    gram_rows = owned_rows[:, :skip_width] / valid_total
    cross_rows = owned_rows[:, skip_width:] * (CLASSES / valid_total)
    return (gram_rows, cross_rows)


def solution(mesh):
    sizes = fine_sizes(mesh.shape["seg"], mesh.shape["utt"])
    fine = Mesh(mesh.devices.reshape(tuple(sizes[n] for n in FINE)), FINE)
    in_specs = (P(UTT, SEG), P(UTT), P(UTT, SEG), P(), P(), P(), P())
    out_specs = (P(FINE, None), P(FINE, None))
    return jax.shard_map(
        per_device, mesh=fine, in_specs=in_specs, out_specs=out_specs, check_vma=False
    )
```

```python
import jax
import jax.numpy as jnp
from jax import lax
from jax.sharding import Mesh, PartitionSpec as P

CLASSES = 256
FRAME = 128


HALF_ROOT = 0.7071067811865476


SEG = ("xl", "core")
UTT = ("y", "xh", "z")
FINE = SEG + UTT
GROUPS = (("core",), ("z",), ("y",), ("xh",), ("xl",))


def linear(index, names, sizes):
    value = 0
    for name in names:
        value = value * sizes[name] + index[name]
    return value


def owner_pairs(sizes):
    import itertools

    pairs = []
    for digits in itertools.product(*(range(sizes[n]) for n in FINE)):
        index = dict(zip(FINE, digits))
        block = 0
        for group in GROUPS:
            size = 1
            for name in group:
                size *= sizes[name]
            block = block * size + linear(index, group, sizes)
        pairs.append((linear(index, FINE, sizes), block))
    return pairs


def fine_sizes(seg_size, utt_size):
    z = 8 if utt_size % 8 == 0 else utt_size
    xh = 2 if (utt_size // z) % 2 == 0 else 1
    return {"xl": seg_size // 2, "core": 2, "y": utt_size // (z * xh), "xh": xh, "z": z}


def shifted(value, axis, by):
    length = 1
    for name in axis:
        length *= lax.axis_size(name)
    pairs = [(i, i + by) for i in range(length) if 0 <= i + by < length]
    return lax.ppermute(value, axis, pairs)


def round_up(value, step):
    return -(-value // step) * step


def layer_math(delayed, current, conv_one, res_one):
    channels = current.shape[1]
    paired = jnp.concatenate([delayed, current], 1)
    preact = jnp.dot(paired, conv_one, preferred_element_type=jnp.float32)
    gate_width = preact.shape[1] // 2
    gated = (jnp.tanh(preact[:, :gate_width]) * jax.nn.sigmoid(preact[:, gate_width:])).astype(
        jnp.bfloat16
    )
    following = None
    if res_one is not None:
        residual_term = jnp.dot(gated, res_one, preferred_element_type=jnp.float32)
        following = ((current.astype(jnp.float32) + residual_term) * HALF_ROOT).astype(
            jnp.bfloat16
        )
    return gated, following


def per_device(
    audio_waves, lengths, target_ids, input_weight, conv_weight, res_weight, skip_weight
):
    batch_rows, seg_len = audio_waves.shape
    layer_total = conv_weight.shape[0]
    reach = 2**layer_total - 1
    earlier = shifted(audio_waves, SEG, 1)
    window = round_up(seg_len + reach, 16)
    extended = jnp.concatenate([earlier, audio_waves], 1)[0, 2 * seg_len - window :]
    hidden = (extended[:, None] * input_weight[None, :]).astype(jnp.bfloat16)
    gated_list = []
    for layer_num in range(layer_total):
        dilation = 2**layer_num
        later_reach = 2**layer_total - 2 ** (layer_num + 1)
        in_len = hidden.shape[0]
        out_len = min(in_len, round_up(seg_len + later_reach, 16))
        if in_len - dilation >= out_len:
            delayed = hidden[in_len - out_len - dilation : in_len - dilation]
        else:
            delayed = jnp.concatenate(
                [jnp.zeros((dilation, hidden.shape[1]), hidden.dtype), hidden[: in_len - dilation]],
                0,
            )
        current = hidden[in_len - out_len :]
        res_one = res_weight[layer_num] if layer_num < layer_total - 1 else None
        gated, hidden = layer_math(delayed, current, conv_weight[layer_num], res_one)
        gated_list.append(gated[out_len - seg_len :])
    stacked = jnp.concatenate(gated_list, 1)
    skip_sum = jnp.dot(stacked, skip_weight, preferred_element_type=jnp.float32)
    features = jnp.maximum(skip_sum, 0.0).astype(jnp.bfloat16)
    skip_width = features.shape[1]
    position = lax.axis_index(SEG) * seg_len + jnp.arange(seg_len, dtype=jnp.int32)
    valid = (position[None, :] < lengths[:, None]).reshape(batch_rows * seg_len)
    masked = jnp.where(valid[:, None], features, jnp.zeros_like(features))
    frame_ids = jnp.repeat(target_ids, FRAME, axis=1).reshape(batch_rows * seg_len)
    onehot = (frame_ids[:, None] == jnp.arange(CLASSES, dtype=jnp.int32)[None, :]).astype(
        jnp.bfloat16
    )
    paired = jnp.concatenate([masked, onehot], 1)
    partial = lax.dot_general(
        masked, paired, (((0,), (0,)), ((), ())), preferred_element_type=jnp.float32
    )
    sizes = {name: lax.axis_size(name) for name in FINE}
    owners = 1
    for name in FINE:
        owners *= sizes[name]
    row_count = partial.shape[0] // owners
    width = partial.shape[1]
    group_sizes = []
    for group in GROUPS:
        size = 1
        for name in group:
            size *= sizes[name]
        group_sizes.append(size)
    local_count = jnp.sum(valid.astype(jnp.float32))
    rows = lax.broadcasted_iota(jnp.int32, partial.shape, 0)
    cols = lax.broadcasted_iota(jnp.int32, partial.shape, 1)
    slot = (rows % row_count == 1) & (cols == rows - 1)
    partial = jnp.where(slot, local_count, partial)
    chunk = (8, row_count * width // 8)
    slab = partial.reshape(tuple(group_sizes) + chunk)
    for stage, group in enumerate(GROUPS):
        slab = lax.psum_scatter(slab, group, scatter_dimension=stage, tiled=True)
    slab = lax.ppermute(slab, FINE, owner_pairs(sizes))
    owned_rows = slab.reshape(row_count, width)
    first_col = lax.axis_index(FINE) * row_count
    valid_total = lax.dynamic_slice(owned_rows, (1, first_col), (1, 1))[0, 0]
    mirror = lax.dynamic_slice(owned_rows, (0, first_col + 1), (1, 1))[0, 0]
    own_rows = lax.broadcasted_iota(jnp.int32, owned_rows.shape, 0)
    own_cols = lax.broadcasted_iota(jnp.int32, owned_rows.shape, 1)
    owned_rows = jnp.where((own_rows == 1) & (own_cols == first_col), mirror, owned_rows)
    gram_rows = owned_rows[:, :skip_width] / valid_total
    cross_rows = owned_rows[:, skip_width:] * (CLASSES / valid_total)
    return (gram_rows, cross_rows)


def solution(mesh):
    sizes = fine_sizes(mesh.shape["seg"], mesh.shape["utt"])
    fine = Mesh(mesh.devices.reshape(tuple(sizes[n] for n in FINE)), FINE)
    in_specs = (P(UTT, SEG), P(UTT), P(UTT, SEG), P(), P(), P(), P())
    out_specs = (P(FINE, None), P(FINE, None))
    return jax.shard_map(
        per_device, mesh=fine, in_specs=in_specs, out_specs=out_specs, check_vma=False
    )
```

```python
import jax
import jax.numpy as jnp
from jax import lax
from jax.sharding import Mesh, PartitionSpec as P

CLASSES = 256
FRAME = 128


HALF_ROOT = 0.7071067811865476


SEG = ("xl", "core")
UTT = ("y", "xh", "z")
FINE = SEG + UTT
GROUPS = (("core",), ("z",), ("y",), ("xh",), ("xl",))
EXCHANGED = ("core", "y", "xh", "xl")


def linear(index, names, sizes):
    value = 0
    for name in names:
        value = value * sizes[name] + index[name]
    return value


def owner_pairs(sizes):
    import itertools

    pairs = []
    for digits in itertools.product(*(range(sizes[n]) for n in FINE)):
        index = dict(zip(FINE, digits))
        block = 0
        for group in GROUPS:
            size = 1
            for name in group:
                size *= sizes[name]
            block = block * size + linear(index, group, sizes)
        pairs.append((linear(index, FINE, sizes), block))
    return pairs


def fine_sizes(seg_size, utt_size):
    z = 8 if utt_size % 8 == 0 else utt_size
    xh = 2 if (utt_size // z) % 2 == 0 else 1
    return {"xl": seg_size // 2, "core": 2, "y": utt_size // (z * xh), "xh": xh, "z": z}


def shifted(value, axis, by):
    length = 1
    for name in axis:
        length *= lax.axis_size(name)
    pairs = [(i, i + by) for i in range(length) if 0 <= i + by < length]
    return lax.ppermute(value, axis, pairs)


def exchange_scatter(slab, axis, dim):
    size = slab.shape[dim]
    index = lax.axis_index(axis)
    bit = size // 2
    while bit >= 1:
        shape = slab.shape
        split = shape[:dim] + (2, shape[dim] // 2) + shape[dim + 1 :]
        halves = slab.reshape(split)
        side = (index // bit) % 2
        mine = lax.dynamic_index_in_dim(halves, side, dim, keepdims=False)
        other = lax.dynamic_index_in_dim(halves, 1 - side, dim, keepdims=False)
        pairs = [(i, i ^ bit) for i in range(size)]
        slab = mine + lax.ppermute(other, axis, pairs)
        bit //= 2
    return slab


def round_up(value, step):
    return -(-value // step) * step


def layer_math(delayed, current, conv_one, res_one):
    channels = current.shape[1]
    paired = jnp.concatenate([delayed, current], 1)
    preact = jnp.dot(paired, conv_one, preferred_element_type=jnp.float32)
    gate_width = preact.shape[1] // 2
    gated = (jnp.tanh(preact[:, :gate_width]) * jax.nn.sigmoid(preact[:, gate_width:])).astype(
        jnp.bfloat16
    )
    following = None
    if res_one is not None:
        residual_term = jnp.dot(gated, res_one, preferred_element_type=jnp.float32)
        following = ((current.astype(jnp.float32) + residual_term) * HALF_ROOT).astype(
            jnp.bfloat16
        )
    return gated, following


def per_device(
    audio_waves, lengths, target_ids, input_weight, conv_weight, res_weight, skip_weight
):
    batch_rows, seg_len = audio_waves.shape
    layer_total = conv_weight.shape[0]
    reach = 2**layer_total - 1
    earlier = shifted(audio_waves, SEG, 1)
    window = round_up(seg_len + reach, 16)
    extended = jnp.concatenate([earlier, audio_waves], 1)[0, 2 * seg_len - window :]
    hidden = (extended[:, None] * input_weight[None, :]).astype(jnp.bfloat16)
    gated_list = []
    for layer_num in range(layer_total):
        dilation = 2**layer_num
        later_reach = 2**layer_total - 2 ** (layer_num + 1)
        in_len = hidden.shape[0]
        out_len = min(in_len, round_up(seg_len + later_reach, 16))
        if in_len - dilation >= out_len:
            delayed = hidden[in_len - out_len - dilation : in_len - dilation]
        else:
            delayed = jnp.concatenate(
                [jnp.zeros((dilation, hidden.shape[1]), hidden.dtype), hidden[: in_len - dilation]],
                0,
            )
        current = hidden[in_len - out_len :]
        res_one = res_weight[layer_num] if layer_num < layer_total - 1 else None
        gated, hidden = layer_math(delayed, current, conv_weight[layer_num], res_one)
        gated_list.append(gated[out_len - seg_len :])
    stacked = jnp.concatenate(gated_list, 1)
    skip_sum = jnp.dot(stacked, skip_weight, preferred_element_type=jnp.float32)
    features = jnp.maximum(skip_sum, 0.0).astype(jnp.bfloat16)
    skip_width = features.shape[1]
    position = lax.axis_index(SEG) * seg_len + jnp.arange(seg_len, dtype=jnp.int32)
    valid = (position[None, :] < lengths[:, None]).reshape(batch_rows * seg_len)
    masked = jnp.where(valid[:, None], features, jnp.zeros_like(features))
    frame_ids = jnp.repeat(target_ids, FRAME, axis=1).reshape(batch_rows * seg_len)
    onehot = (frame_ids[:, None] == jnp.arange(CLASSES, dtype=jnp.int32)[None, :]).astype(
        jnp.bfloat16
    )
    paired = jnp.concatenate([masked, onehot], 1)
    partial = lax.dot_general(
        masked, paired, (((0,), (0,)), ((), ())), preferred_element_type=jnp.float32
    )
    sizes = {name: lax.axis_size(name) for name in FINE}
    owners = 1
    for name in FINE:
        owners *= sizes[name]
    row_count = partial.shape[0] // owners
    width = partial.shape[1]
    group_sizes = []
    for group in GROUPS:
        size = 1
        for name in group:
            size *= sizes[name]
        group_sizes.append(size)
    local_count = jnp.sum(valid.astype(jnp.float32))
    rows = lax.broadcasted_iota(jnp.int32, partial.shape, 0)
    cols = lax.broadcasted_iota(jnp.int32, partial.shape, 1)
    slot = (rows % row_count == 1) & (cols == rows - 1)
    partial = jnp.where(slot, local_count, partial)
    chunk = (8, row_count * width // 8)
    slab = partial.reshape(tuple(group_sizes) + chunk)
    for stage, group in enumerate(GROUPS):
        if group[0] in EXCHANGED and len(group) == 1:
            slab = exchange_scatter(slab, group[0], stage)
        else:
            slab = lax.psum_scatter(slab, group, scatter_dimension=stage, tiled=True)
    slab = lax.ppermute(slab, FINE, owner_pairs(sizes))
    owned_rows = slab.reshape(row_count, width)
    first_col = lax.axis_index(FINE) * row_count
    valid_total = lax.dynamic_slice(owned_rows, (1, first_col), (1, 1))[0, 0]
    mirror = lax.dynamic_slice(owned_rows, (0, first_col + 1), (1, 1))[0, 0]
    own_rows = lax.broadcasted_iota(jnp.int32, owned_rows.shape, 0)
    own_cols = lax.broadcasted_iota(jnp.int32, owned_rows.shape, 1)
    owned_rows = jnp.where((own_rows == 1) & (own_cols == first_col), mirror, owned_rows)
    gram_rows = owned_rows[:, :skip_width] / valid_total
    cross_rows = owned_rows[:, skip_width:] * (CLASSES / valid_total)
    return (gram_rows, cross_rows)


def solution(mesh):
    sizes = fine_sizes(mesh.shape["seg"], mesh.shape["utt"])
    fine = Mesh(mesh.devices.reshape(tuple(sizes[n] for n in FINE)), FINE)
    in_specs = (P(UTT, SEG), P(UTT), P(UTT, SEG), P(), P(), P(), P())
    out_specs = (P(FINE, None), P(FINE, None))
    return jax.shard_map(
        per_device, mesh=fine, in_specs=in_specs, out_specs=out_specs, check_vma=False
    )
```

```python
import jax
import jax.numpy as jnp
from jax import lax
from jax.sharding import Mesh, PartitionSpec as P

CLASSES = 256
FRAME = 128


HALF_ROOT = 0.7071067811865476


SEG = ("xl", "core")
UTT = ("y", "xh", "z")
FINE = SEG + UTT
GROUPS = (("core",), ("z",), ("y",), ("xh",), ("xl",))
EXCHANGED = ("core", "y", "xh", "xl")


def linear(index, names, sizes):
    value = 0
    for name in names:
        value = value * sizes[name] + index[name]
    return value


def owner_pairs(sizes):
    import itertools

    pairs = []
    for digits in itertools.product(*(range(sizes[n]) for n in FINE)):
        index = dict(zip(FINE, digits))
        block = 0
        for group in GROUPS:
            size = 1
            for name in group:
                size *= sizes[name]
            block = block * size + linear(index, group, sizes)
        pairs.append((linear(index, FINE, sizes), block))
    return pairs


def fine_sizes(seg_size, utt_size):
    z = 8 if utt_size % 8 == 0 else utt_size
    xh = 2 if (utt_size // z) % 2 == 0 else 1
    return {"xl": seg_size // 2, "core": 2, "y": utt_size // (z * xh), "xh": xh, "z": z}


def shifted(value, axis, by):
    length = 1
    for name in axis:
        length *= lax.axis_size(name)
    pairs = [(i, i + by) for i in range(length) if 0 <= i + by < length]
    return lax.ppermute(value, axis, pairs)


def exchange_scatter(slab, axis, dim):
    size = slab.shape[dim]
    index = lax.axis_index(axis)
    bit = size // 2
    while bit >= 1:
        shape = slab.shape
        split = shape[:dim] + (2, shape[dim] // 2) + shape[dim + 1 :]
        halves = slab.reshape(split)
        side = (index // bit) % 2
        mine = lax.dynamic_index_in_dim(halves, side, dim, keepdims=False)
        other = lax.dynamic_index_in_dim(halves, 1 - side, dim, keepdims=False)
        pairs = [(i, i ^ bit) for i in range(size)]
        slab = mine + lax.ppermute(other, axis, pairs)
        bit //= 2
    return slab


def round_up(value, step):
    return -(-value // step) * step


def layer_math(delayed, current, conv_one, res_one):
    channels = current.shape[1]
    paired = jnp.concatenate([delayed, current], 1)
    preact = jnp.dot(paired, conv_one, preferred_element_type=jnp.float32)
    gate_width = preact.shape[1] // 2
    gated = (jnp.tanh(preact[:, :gate_width]) * jax.nn.sigmoid(preact[:, gate_width:])).astype(
        jnp.bfloat16
    )
    following = None
    if res_one is not None:
        residual_term = jnp.dot(gated, res_one, preferred_element_type=jnp.float32)
        following = ((current.astype(jnp.float32) + residual_term) * HALF_ROOT).astype(
            jnp.bfloat16
        )
    return gated, following


def per_device(
    audio_waves, lengths, target_ids, input_weight, conv_weight, res_weight, skip_weight
):
    batch_rows, seg_len = audio_waves.shape
    layer_total = conv_weight.shape[0]
    reach = 2**layer_total - 1
    earlier = shifted(audio_waves, SEG, 1)
    window = round_up(seg_len + reach, 16)
    extended = jnp.concatenate([earlier, audio_waves], 1)[0, 2 * seg_len - window :]
    hidden = (extended[:, None] * input_weight[None, :]).astype(jnp.bfloat16)
    gated_list = []
    for layer_num in range(layer_total):
        dilation = 2**layer_num
        later_reach = 2**layer_total - 2 ** (layer_num + 1)
        in_len = hidden.shape[0]
        out_len = min(in_len, round_up(seg_len + later_reach, 16))
        if in_len - dilation >= out_len:
            delayed = hidden[in_len - out_len - dilation : in_len - dilation]
        else:
            delayed = jnp.concatenate(
                [jnp.zeros((dilation, hidden.shape[1]), hidden.dtype), hidden[: in_len - dilation]],
                0,
            )
        current = hidden[in_len - out_len :]
        res_one = res_weight[layer_num] if layer_num < layer_total - 1 else None
        gated, hidden = layer_math(delayed, current, conv_weight[layer_num], res_one)
        gated_list.append(gated[out_len - seg_len :])
    stacked = jnp.concatenate(gated_list, 1)
    skip_sum = jnp.dot(stacked, skip_weight, preferred_element_type=jnp.float32)
    features = jnp.maximum(skip_sum, 0.0).astype(jnp.bfloat16)
    skip_width = features.shape[1]
    position = lax.axis_index(SEG) * seg_len + jnp.arange(seg_len, dtype=jnp.int32)
    valid = (position[None, :] < lengths[:, None]).reshape(batch_rows * seg_len)
    masked = jnp.where(valid[:, None], features, jnp.zeros_like(features))
    frame_ids = jnp.repeat(target_ids, FRAME, axis=1).reshape(batch_rows * seg_len)
    onehot = (frame_ids[:, None] == jnp.arange(CLASSES, dtype=jnp.int32)[None, :]).astype(
        jnp.bfloat16
    )
    paired = jnp.concatenate([masked, onehot], 1)
    partial = lax.dot_general(
        masked, paired, (((0,), (0,)), ((), ())), preferred_element_type=jnp.float32
    )
    sizes = {name: lax.axis_size(name) for name in FINE}
    owners = 1
    for name in FINE:
        owners *= sizes[name]
    row_count = partial.shape[0] // owners
    width = partial.shape[1]
    group_sizes = []
    for group in GROUPS:
        size = 1
        for name in group:
            size *= sizes[name]
        group_sizes.append(size)
    local_count = jnp.sum(valid.astype(jnp.float32))
    rows = lax.broadcasted_iota(jnp.int32, partial.shape, 0)
    cols = lax.broadcasted_iota(jnp.int32, partial.shape, 1)
    slot = (rows % row_count == 1) & (cols == rows - 1)
    partial = jnp.where(slot, local_count, partial)
    pair = group_sizes[-1] * row_count
    slab = partial.reshape(tuple(group_sizes[:-1]) + (pair, width))
    for stage, group in enumerate(GROUPS):
        if stage == len(GROUPS) - 1:
            slab = slab.reshape(tuple(slab.shape[:-2]) + (group_sizes[-1], row_count, width))
        if group[0] in EXCHANGED and len(group) == 1:
            slab = exchange_scatter(slab, group[0], stage)
        else:
            slab = lax.psum_scatter(slab, group, scatter_dimension=stage, tiled=True)
    slab = lax.ppermute(slab, FINE, owner_pairs(sizes))
    owned_rows = slab.reshape(row_count, width)
    first_col = lax.axis_index(FINE) * row_count
    valid_total = lax.dynamic_slice(owned_rows, (1, first_col), (1, 1))[0, 0]
    mirror = lax.dynamic_slice(owned_rows, (0, first_col + 1), (1, 1))[0, 0]
    own_rows = lax.broadcasted_iota(jnp.int32, owned_rows.shape, 0)
    own_cols = lax.broadcasted_iota(jnp.int32, owned_rows.shape, 1)
    owned_rows = jnp.where((own_rows == 1) & (own_cols == first_col), mirror, owned_rows)
    gram_rows = owned_rows[:, :skip_width] / valid_total
    cross_rows = owned_rows[:, skip_width:] * (CLASSES / valid_total)
    return (gram_rows, cross_rows)


def solution(mesh):
    sizes = fine_sizes(mesh.shape["seg"], mesh.shape["utt"])
    fine = Mesh(mesh.devices.reshape(tuple(sizes[n] for n in FINE)), FINE)
    in_specs = (P(UTT, SEG), P(UTT), P(UTT, SEG), P(), P(), P(), P())
    out_specs = (P(FINE, None), P(FINE, None))
    return jax.shard_map(
        per_device, mesh=fine, in_specs=in_specs, out_specs=out_specs, check_vma=False
    )
```

```python
import os

import jax
import jax.numpy as jnp
from jax import lax
from jax.experimental import pallas as pl
from jax.experimental.pallas import tpu as pltpu
from jax.sharding import Mesh, PartitionSpec as P

CLASSES = 256
FRAME = 128


HALF_ROOT = 0.7071067811865476


SEG = ("xl", "core")
UTT = ("y", "xh", "z")
FINE = SEG + UTT
GROUPS = (("core",), ("z",), ("y",), ("xh",), ("xl",))
EXCHANGED = ("core", "y", "xh", "xl")


def linear(index, names, sizes):
    value = 0
    for name in names:
        value = value * sizes[name] + index[name]
    return value


def owner_pairs(sizes):
    import itertools

    pairs = []
    for digits in itertools.product(*(range(sizes[n]) for n in FINE)):
        index = dict(zip(FINE, digits))
        block = 0
        for group in GROUPS:
            size = 1
            for name in group:
                size *= sizes[name]
            block = block * size + linear(index, group, sizes)
        pairs.append((linear(index, FINE, sizes), block))
    return pairs


def fine_sizes(seg_size, utt_size):
    z = 8 if utt_size % 8 == 0 else utt_size
    xh = 2 if (utt_size // z) % 2 == 0 else 1
    return {"xl": seg_size // 2, "core": 2, "y": utt_size // (z * xh), "xh": xh, "z": z}


def shifted(value, axis, by):
    length = 1
    for name in axis:
        length *= lax.axis_size(name)
    pairs = [(i, i + by) for i in range(length) if 0 <= i + by < length]
    return lax.ppermute(value, axis, pairs)


def exchange_scatter(slab, axis, dim):
    size = slab.shape[dim]
    index = lax.axis_index(axis)
    bit = size // 2
    while bit >= 1:
        shape = slab.shape
        split = shape[:dim] + (2, shape[dim] // 2) + shape[dim + 1 :]
        halves = slab.reshape(split)
        side = (index // bit) % 2
        mine = lax.dynamic_index_in_dim(halves, side, dim, keepdims=False)
        other = lax.dynamic_index_in_dim(halves, 1 - side, dim, keepdims=False)
        pairs = [(i, i ^ bit) for i in range(size)]
        slab = mine + lax.ppermute(other, axis, pairs)
        bit //= 2
    return slab


CHUNK = 256
FRONT = 512


def layers_kernel(h0_ref, conv_ref, res_ref, out_ref, buf_a, buf_b):
    window = h0_ref.shape[0]
    seg_len = out_ref.shape[0]
    layer_total = conv_ref.shape[0]
    gate = conv_ref.shape[2] // 2
    buf_a[0:FRONT, :] = jnp.zeros((FRONT, buf_a.shape[1]), jnp.float32)
    buf_b[0:FRONT, :] = jnp.zeros((FRONT, buf_b.shape[1]), jnp.float32)
    buf_a[FRONT:, :] = h0_ref[...].astype(jnp.float32)
    bufs = (buf_a, buf_b)
    for layer_num in range(layer_total):
        dilation = 2**layer_num
        later_reach = 2**layer_total - 2 ** (layer_num + 1)
        needed = round_up(seg_len + later_reach, CHUNK)
        first_chunk = max(0, (window - needed) // CHUNK)
        src = bufs[layer_num % 2]
        dst = bufs[(layer_num + 1) % 2]
        conv_one = conv_ref[layer_num]
        res_one = res_ref[layer_num] if layer_num < layer_total - 1 else None

        def body(chunk, carry, src=src, dst=dst, dilation=dilation, conv_one=conv_one,
                 res_one=res_one, layer_num=layer_num):
            start = pl.multiple_of(FRONT + chunk * CHUNK, CHUNK)
            current = src[pl.ds(start, CHUNK), :]
            if dilation % 8 == 0:
                delayed = src[pl.ds(start - dilation, CHUNK), :]
            else:
                wide = src[pl.ds(start - 8, CHUNK + 8), :]
                delayed = pltpu.roll(wide, dilation, 0)[8:, :]
            paired = jnp.concatenate(
                [delayed.astype(jnp.bfloat16), current.astype(jnp.bfloat16)], 1
            )
            preact = jnp.dot(paired, conv_one, preferred_element_type=jnp.float32)
            gated = (jnp.tanh(preact[:, :gate]) * jax.nn.sigmoid(preact[:, gate:])).astype(
                jnp.bfloat16
            )

            @pl.when(chunk * CHUNK >= window - seg_len)
            def _():
                row = pl.multiple_of(chunk * CHUNK - (window - seg_len), CHUNK)
                out_ref[pl.ds(row, CHUNK), layer_num * gate : (layer_num + 1) * gate] = gated

            if res_one is not None:
                residual_term = jnp.dot(gated, res_one, preferred_element_type=jnp.float32)
                following = ((current + residual_term) * HALF_ROOT).astype(jnp.bfloat16)
                dst[pl.ds(start, CHUNK), :] = following.astype(jnp.float32)
            return carry

        lax.fori_loop(first_chunk, window // CHUNK, body, 0)


def run_layers(h0, conv_weight, res_weight, seg_len):
    window, channels = h0.shape
    layer_total, _, both = conv_weight.shape
    return pl.pallas_call(
        layers_kernel,
        out_shape=jax.ShapeDtypeStruct((seg_len, layer_total * both // 2), jnp.bfloat16),
        scratch_shapes=[
            pltpu.VMEM((FRONT + window, channels), jnp.float32),
            pltpu.VMEM((FRONT + window, channels), jnp.float32),
        ],
        interpret=bool(os.environ.get("SOLUTION_INTERPRET")),
    )(h0, conv_weight, res_weight)


def round_up(value, step):
    return -(-value // step) * step


def layer_math(delayed, current, conv_one, res_one):
    channels = current.shape[1]
    paired = jnp.concatenate([delayed, current], 1)
    preact = jnp.dot(paired, conv_one, preferred_element_type=jnp.float32)
    gate_width = preact.shape[1] // 2
    gated = (jnp.tanh(preact[:, :gate_width]) * jax.nn.sigmoid(preact[:, gate_width:])).astype(
        jnp.bfloat16
    )
    following = None
    if res_one is not None:
        residual_term = jnp.dot(gated, res_one, preferred_element_type=jnp.float32)
        following = ((current.astype(jnp.float32) + residual_term) * HALF_ROOT).astype(
            jnp.bfloat16
        )
    return gated, following


def per_device(
    audio_waves, lengths, target_ids, input_weight, conv_weight, res_weight, skip_weight
):
    batch_rows, seg_len = audio_waves.shape
    layer_total = conv_weight.shape[0]
    reach = 2**layer_total - 1
    earlier = shifted(audio_waves, SEG, 1)
    window = round_up(seg_len + reach, CHUNK)
    extended = jnp.concatenate([earlier, audio_waves], 1)[0, 2 * seg_len - window :]
    hidden = (extended[:, None] * input_weight[None, :]).astype(jnp.bfloat16)
    stacked = run_layers(hidden, conv_weight, res_weight, seg_len)
    skip_sum = jnp.dot(stacked, skip_weight, preferred_element_type=jnp.float32)
    features = jnp.maximum(skip_sum, 0.0).astype(jnp.bfloat16)
    skip_width = features.shape[1]
    position = lax.axis_index(SEG) * seg_len + jnp.arange(seg_len, dtype=jnp.int32)
    valid = (position[None, :] < lengths[:, None]).reshape(batch_rows * seg_len)
    masked = jnp.where(valid[:, None], features, jnp.zeros_like(features))
    frame_ids = jnp.repeat(target_ids, FRAME, axis=1).reshape(batch_rows * seg_len)
    onehot = (frame_ids[:, None] == jnp.arange(CLASSES, dtype=jnp.int32)[None, :]).astype(
        jnp.bfloat16
    )
    paired = jnp.concatenate([masked, onehot], 1)
    partial = lax.dot_general(
        masked, paired, (((0,), (0,)), ((), ())), preferred_element_type=jnp.float32
    )
    sizes = {name: lax.axis_size(name) for name in FINE}
    owners = 1
    for name in FINE:
        owners *= sizes[name]
    row_count = partial.shape[0] // owners
    width = partial.shape[1]
    group_sizes = []
    for group in GROUPS:
        size = 1
        for name in group:
            size *= sizes[name]
        group_sizes.append(size)
    local_count = jnp.sum(valid.astype(jnp.float32))
    rows = lax.broadcasted_iota(jnp.int32, partial.shape, 0)
    cols = lax.broadcasted_iota(jnp.int32, partial.shape, 1)
    slot = (rows % row_count == 1) & (cols == rows - 1)
    partial = jnp.where(slot, local_count, partial)
    pair = group_sizes[-1] * row_count
    slab = partial.reshape(tuple(group_sizes[:-1]) + (pair, width))
    for stage, group in enumerate(GROUPS):
        if stage == len(GROUPS) - 1:
            slab = slab.reshape(tuple(slab.shape[:-2]) + (group_sizes[-1], row_count, width))
        if group[0] in EXCHANGED and len(group) == 1:
            slab = exchange_scatter(slab, group[0], stage)
        else:
            slab = lax.psum_scatter(slab, group, scatter_dimension=stage, tiled=True)
    slab = lax.ppermute(slab, FINE, owner_pairs(sizes))
    owned_rows = slab.reshape(row_count, width)
    first_col = lax.axis_index(FINE) * row_count
    valid_total = lax.dynamic_slice(owned_rows, (1, first_col), (1, 1))[0, 0]
    mirror = lax.dynamic_slice(owned_rows, (0, first_col + 1), (1, 1))[0, 0]
    own_rows = lax.broadcasted_iota(jnp.int32, owned_rows.shape, 0)
    own_cols = lax.broadcasted_iota(jnp.int32, owned_rows.shape, 1)
    owned_rows = jnp.where((own_rows == 1) & (own_cols == first_col), mirror, owned_rows)
    gram_rows = owned_rows[:, :skip_width] / valid_total
    cross_rows = owned_rows[:, skip_width:] * (CLASSES / valid_total)
    return (gram_rows, cross_rows)


def solution(mesh):
    sizes = fine_sizes(mesh.shape["seg"], mesh.shape["utt"])
    fine = Mesh(mesh.devices.reshape(tuple(sizes[n] for n in FINE)), FINE)
    in_specs = (P(UTT, SEG), P(UTT), P(UTT, SEG), P(), P(), P(), P())
    out_specs = (P(FINE, None), P(FINE, None))
    return jax.shard_map(
        per_device, mesh=fine, in_specs=in_specs, out_specs=out_specs, check_vma=False
    )
```

```python
import jax
import jax.numpy as jnp
from jax import lax
from jax.sharding import Mesh, PartitionSpec as P

CLASSES = 256
FRAME = 128


HALF_ROOT = 0.7071067811865476


SEG = ("xl", "core")
UTT = ("y", "xh", "z")
FINE = SEG + UTT
GROUPS = (("core",), ("z",), ("y",), ("xh",), ("xl",))
EXCHANGED = ("core", "y", "xh", "xl")


def linear(index, names, sizes):
    value = 0
    for name in names:
        value = value * sizes[name] + index[name]
    return value


def owner_pairs(sizes):
    import itertools

    pairs = []
    for digits in itertools.product(*(range(sizes[n]) for n in FINE)):
        index = dict(zip(FINE, digits))
        block = 0
        for group in GROUPS:
            size = 1
            for name in group:
                size *= sizes[name]
            block = block * size + linear(index, group, sizes)
        pairs.append((linear(index, FINE, sizes), block))
    return pairs


def fine_sizes(seg_size, utt_size):
    z = 8 if utt_size % 8 == 0 else utt_size
    xh = 2 if (utt_size // z) % 2 == 0 else 1
    return {"xl": seg_size // 2, "core": 2, "y": utt_size // (z * xh), "xh": xh, "z": z}


def shifted(value, axis, by):
    length = 1
    for name in axis:
        length *= lax.axis_size(name)
    pairs = [(i, i + by) for i in range(length) if 0 <= i + by < length]
    return lax.ppermute(value, axis, pairs)


def exchange_scatter(slab, axis, dim):
    size = slab.shape[dim]
    index = lax.axis_index(axis)
    bit = size // 2
    while bit >= 1:
        shape = slab.shape
        split = shape[:dim] + (2, shape[dim] // 2) + shape[dim + 1 :]
        halves = slab.reshape(split)
        side = (index // bit) % 2
        mine = lax.dynamic_index_in_dim(halves, side, dim, keepdims=False)
        other = lax.dynamic_index_in_dim(halves, 1 - side, dim, keepdims=False)
        pairs = [(i, i ^ bit) for i in range(size)]
        slab = mine + lax.ppermute(other, axis, pairs)
        bit //= 2
    return slab


def round_up(value, step):
    return -(-value // step) * step


def layer_math(delayed, current, conv_one, res_one):
    channels = current.shape[1]
    paired = jnp.concatenate([delayed, current], 1)
    preact = jnp.dot(paired, conv_one, preferred_element_type=jnp.float32)
    gate_width = preact.shape[1] // 2
    gated = (jnp.tanh(preact[:, :gate_width]) * jax.nn.sigmoid(preact[:, gate_width:])).astype(
        jnp.bfloat16
    )
    following = None
    if res_one is not None:
        residual_term = jnp.dot(gated, res_one, preferred_element_type=jnp.float32)
        following = ((current.astype(jnp.float32) + residual_term) * HALF_ROOT).astype(
            jnp.bfloat16
        )
    return gated, following


def per_device(
    audio_waves, lengths, target_ids, input_weight, conv_weight, res_weight, skip_weight
):
    batch_rows, seg_len = audio_waves.shape
    layer_total = conv_weight.shape[0]
    reach = 2**layer_total - 1
    earlier = shifted(audio_waves, SEG, 1)
    window = round_up(seg_len + reach, 16)
    extended = jnp.concatenate([earlier, audio_waves], 1)[0, 2 * seg_len - window :]
    hidden = (extended[:, None] * input_weight[None, :]).astype(jnp.bfloat16)
    gated_list = []
    for layer_num in range(layer_total):
        dilation = 2**layer_num
        later_reach = 2**layer_total - 2 ** (layer_num + 1)
        in_len = hidden.shape[0]
        out_len = min(in_len, round_up(seg_len + later_reach, 16))
        if in_len - dilation >= out_len:
            delayed = hidden[in_len - out_len - dilation : in_len - dilation]
        else:
            delayed = jnp.concatenate(
                [jnp.zeros((dilation, hidden.shape[1]), hidden.dtype), hidden[: in_len - dilation]],
                0,
            )
        current = hidden[in_len - out_len :]
        res_one = res_weight[layer_num] if layer_num < layer_total - 1 else None
        gated, hidden = layer_math(delayed, current, conv_weight[layer_num], res_one)
        gated_list.append(gated[out_len - seg_len :])
    stacked = jnp.concatenate(gated_list, 1)
    skip_sum = jnp.dot(stacked, skip_weight, preferred_element_type=jnp.float32)
    features = jnp.maximum(skip_sum, 0.0).astype(jnp.bfloat16)
    skip_width = features.shape[1]
    position = lax.axis_index(SEG) * seg_len + jnp.arange(seg_len, dtype=jnp.int32)
    valid = (position[None, :] < lengths[:, None]).reshape(batch_rows * seg_len)
    masked = jnp.where(valid[:, None], features, jnp.zeros_like(features))
    frame_ids = jnp.repeat(target_ids, FRAME, axis=1).reshape(batch_rows * seg_len)
    onehot = (frame_ids[:, None] == jnp.arange(CLASSES, dtype=jnp.int32)[None, :]).astype(
        jnp.bfloat16
    )
    paired = jnp.concatenate([masked, onehot], 1)
    partial = lax.dot_general(
        masked, paired, (((0,), (0,)), ((), ())), preferred_element_type=jnp.float32
    )
    sizes = {name: lax.axis_size(name) for name in FINE}
    owners = 1
    for name in FINE:
        owners *= sizes[name]
    row_count = partial.shape[0] // owners
    width = partial.shape[1]
    group_sizes = []
    for group in GROUPS:
        size = 1
        for name in group:
            size *= sizes[name]
        group_sizes.append(size)
    local_count = jnp.sum(valid.astype(jnp.float32))
    rows = lax.broadcasted_iota(jnp.int32, partial.shape, 0)
    cols = lax.broadcasted_iota(jnp.int32, partial.shape, 1)
    slot = (rows % row_count == 1) & (cols == rows - 1)
    partial = jnp.where(slot, local_count, partial)
    pair = group_sizes[-1] * row_count
    slab = partial.reshape(tuple(group_sizes[:-1]) + (pair, width))
    slab = exchange_scatter(slab, "core", 0)
    half = width // 2
    left = lax.psum_scatter(slab[..., :half], "z", scatter_dimension=1, tiled=True)
    right = exchange_scatter(slab[..., half:], "y", 2)
    left = exchange_scatter(left, "y", 2)
    right = lax.psum_scatter(right, "z", scatter_dimension=1, tiled=True)
    slab = jnp.concatenate([left, right], -1)
    slab = exchange_scatter(slab, "xh", 3)
    slab = slab.reshape(tuple(slab.shape[:-2]) + (group_sizes[-1], row_count, width))
    slab = exchange_scatter(slab, "xl", 4)
    slab = lax.ppermute(slab, FINE, owner_pairs(sizes))
    owned_rows = slab.reshape(row_count, width)
    first_col = lax.axis_index(FINE) * row_count
    valid_total = lax.dynamic_slice(owned_rows, (1, first_col), (1, 1))[0, 0]
    mirror = lax.dynamic_slice(owned_rows, (0, first_col + 1), (1, 1))[0, 0]
    own_rows = lax.broadcasted_iota(jnp.int32, owned_rows.shape, 0)
    own_cols = lax.broadcasted_iota(jnp.int32, owned_rows.shape, 1)
    owned_rows = jnp.where((own_rows == 1) & (own_cols == first_col), mirror, owned_rows)
    gram_rows = owned_rows[:, :skip_width] / valid_total
    cross_rows = owned_rows[:, skip_width:] * (CLASSES / valid_total)
    return (gram_rows, cross_rows)


def solution(mesh):
    sizes = fine_sizes(mesh.shape["seg"], mesh.shape["utt"])
    fine = Mesh(mesh.devices.reshape(tuple(sizes[n] for n in FINE)), FINE)
    in_specs = (P(UTT, SEG), P(UTT), P(UTT, SEG), P(), P(), P(), P())
    out_specs = (P(FINE, None), P(FINE, None))
    return jax.shard_map(
        per_device, mesh=fine, in_specs=in_specs, out_specs=out_specs, check_vma=False
    )
```

```python
import jax
import jax.numpy as jnp
from jax import lax
from jax.sharding import Mesh, PartitionSpec as P

CLASSES = 256
FRAME = 128


HALF_ROOT = 0.7071067811865476


SEG = ("xl", "core")
UTT = ("y", "xh", "z")
FINE = SEG + UTT
GROUPS = (("core",), ("z",), ("y",), ("xh",), ("xl",))
EXCHANGED = ("core", "y", "xh", "xl")


def linear(index, names, sizes):
    value = 0
    for name in names:
        value = value * sizes[name] + index[name]
    return value


def owner_pairs(sizes):
    import itertools

    pairs = []
    for digits in itertools.product(*(range(sizes[n]) for n in FINE)):
        index = dict(zip(FINE, digits))
        block = 0
        for group in GROUPS:
            size = 1
            for name in group:
                size *= sizes[name]
            block = block * size + reverse_bits(linear(index, group, sizes), size)
        pairs.append((linear(index, FINE, sizes), block))
    return pairs


def fine_sizes(seg_size, utt_size):
    z = 8 if utt_size % 8 == 0 else utt_size
    xh = 2 if (utt_size // z) % 2 == 0 else 1
    return {"xl": seg_size // 2, "core": 2, "y": utt_size // (z * xh), "xh": xh, "z": z}


def shifted(value, axis, by):
    length = 1
    for name in axis:
        length *= lax.axis_size(name)
    pairs = [(i, i + by) for i in range(length) if 0 <= i + by < length]
    return lax.ppermute(value, axis, pairs)


def reverse_bits(value, size):
    result = 0
    bit = 1
    while bit < size:
        result = result * 2 + (value // bit) % 2
        bit *= 2
    return result


def exchange_scatter(slab, axis, dim):
    size = slab.shape[dim]
    index = reverse_bits(lax.axis_index(axis), size)
    bit = size // 2
    while bit >= 1:
        shape = slab.shape
        split = shape[:dim] + (2, shape[dim] // 2) + shape[dim + 1 :]
        halves = slab.reshape(split)
        side = (index // bit) % 2
        mine = lax.dynamic_index_in_dim(halves, side, dim, keepdims=False)
        other = lax.dynamic_index_in_dim(halves, 1 - side, dim, keepdims=False)
        flip = reverse_bits(bit, size)
        pairs = [(i, i ^ flip) for i in range(size)]
        slab = mine + lax.ppermute(other, axis, pairs)
        bit //= 2
    return slab


def round_up(value, step):
    return -(-value // step) * step


def layer_math(delayed, current, conv_one, res_one):
    channels = current.shape[1]
    paired = jnp.concatenate([delayed, current], 1)
    preact = jnp.dot(paired, conv_one, preferred_element_type=jnp.float32)
    gate_width = preact.shape[1] // 2
    gated = (jnp.tanh(preact[:, :gate_width]) * jax.nn.sigmoid(preact[:, gate_width:])).astype(
        jnp.bfloat16
    )
    following = None
    if res_one is not None:
        residual_term = jnp.dot(gated, res_one, preferred_element_type=jnp.float32)
        following = ((current.astype(jnp.float32) + residual_term) * HALF_ROOT).astype(
            jnp.bfloat16
        )
    return gated, following


def per_device(
    audio_waves, lengths, target_ids, input_weight, conv_weight, res_weight, skip_weight
):
    batch_rows, seg_len = audio_waves.shape
    layer_total = conv_weight.shape[0]
    reach = 2**layer_total - 1
    earlier = shifted(audio_waves, SEG, 1)
    window = round_up(seg_len + reach, 16)
    extended = jnp.concatenate([earlier, audio_waves], 1)[0, 2 * seg_len - window :]
    hidden = (extended[:, None] * input_weight[None, :]).astype(jnp.bfloat16)
    gated_list = []
    for layer_num in range(layer_total):
        dilation = 2**layer_num
        later_reach = 2**layer_total - 2 ** (layer_num + 1)
        in_len = hidden.shape[0]
        out_len = min(in_len, round_up(seg_len + later_reach, 16))
        if in_len - dilation >= out_len:
            delayed = hidden[in_len - out_len - dilation : in_len - dilation]
        else:
            delayed = jnp.concatenate(
                [jnp.zeros((dilation, hidden.shape[1]), hidden.dtype), hidden[: in_len - dilation]],
                0,
            )
        current = hidden[in_len - out_len :]
        res_one = res_weight[layer_num] if layer_num < layer_total - 1 else None
        gated, hidden = layer_math(delayed, current, conv_weight[layer_num], res_one)
        gated_list.append(gated[out_len - seg_len :])
    stacked = jnp.concatenate(gated_list, 1)
    skip_sum = jnp.dot(stacked, skip_weight, preferred_element_type=jnp.float32)
    features = jnp.maximum(skip_sum, 0.0).astype(jnp.bfloat16)
    skip_width = features.shape[1]
    position = lax.axis_index(SEG) * seg_len + jnp.arange(seg_len, dtype=jnp.int32)
    valid = (position[None, :] < lengths[:, None]).reshape(batch_rows * seg_len)
    masked = jnp.where(valid[:, None], features, jnp.zeros_like(features))
    frame_ids = jnp.repeat(target_ids, FRAME, axis=1).reshape(batch_rows * seg_len)
    onehot = (frame_ids[:, None] == jnp.arange(CLASSES, dtype=jnp.int32)[None, :]).astype(
        jnp.bfloat16
    )
    paired = jnp.concatenate([masked, onehot], 1)
    partial = lax.dot_general(
        masked, paired, (((0,), (0,)), ((), ())), preferred_element_type=jnp.float32
    )
    sizes = {name: lax.axis_size(name) for name in FINE}
    owners = 1
    for name in FINE:
        owners *= sizes[name]
    row_count = partial.shape[0] // owners
    width = partial.shape[1]
    group_sizes = []
    for group in GROUPS:
        size = 1
        for name in group:
            size *= sizes[name]
        group_sizes.append(size)
    local_count = jnp.sum(valid.astype(jnp.float32))
    rows = lax.broadcasted_iota(jnp.int32, partial.shape, 0)
    cols = lax.broadcasted_iota(jnp.int32, partial.shape, 1)
    slot = (rows % row_count == 1) & (cols == rows - 1)
    partial = jnp.where(slot, local_count, partial)
    pair = group_sizes[-1] * row_count
    slab = partial.reshape(tuple(group_sizes[:-1]) + (pair, width))
    slab = exchange_scatter(slab, "core", 0)
    half = width // 2
    left = exchange_scatter(slab[..., :half], "z", 1)
    right = exchange_scatter(slab[..., half:], "y", 2)
    left = exchange_scatter(left, "y", 2)
    right = exchange_scatter(right, "z", 1)
    slab = jnp.concatenate([left, right], -1)
    slab = exchange_scatter(slab, "xh", 3)
    slab = slab.reshape(tuple(slab.shape[:-2]) + (group_sizes[-1], row_count, width))
    slab = exchange_scatter(slab, "xl", 4)
    slab = lax.ppermute(slab, FINE, owner_pairs(sizes))
    owned_rows = slab.reshape(row_count, width)
    first_col = lax.axis_index(FINE) * row_count
    valid_total = lax.dynamic_slice(owned_rows, (1, first_col), (1, 1))[0, 0]
    mirror = lax.dynamic_slice(owned_rows, (0, first_col + 1), (1, 1))[0, 0]
    own_rows = lax.broadcasted_iota(jnp.int32, owned_rows.shape, 0)
    own_cols = lax.broadcasted_iota(jnp.int32, owned_rows.shape, 1)
    owned_rows = jnp.where((own_rows == 1) & (own_cols == first_col), mirror, owned_rows)
    gram_rows = owned_rows[:, :skip_width] / valid_total
    cross_rows = owned_rows[:, skip_width:] * (CLASSES / valid_total)
    return (gram_rows, cross_rows)


def solution(mesh):
    sizes = fine_sizes(mesh.shape["seg"], mesh.shape["utt"])
    fine = Mesh(mesh.devices.reshape(tuple(sizes[n] for n in FINE)), FINE)
    in_specs = (P(UTT, SEG), P(UTT), P(UTT, SEG), P(), P(), P(), P())
    out_specs = (P(FINE, None), P(FINE, None))
    return jax.shard_map(
        per_device, mesh=fine, in_specs=in_specs, out_specs=out_specs, check_vma=False
    )
```

```python
import jax
import jax.numpy as jnp
from jax import lax
from jax.sharding import Mesh, PartitionSpec as P

CLASSES = 256
FRAME = 128


HALF_ROOT = 0.7071067811865476


SEG = ("xl", "core")
UTT = ("y", "xh", "z")
FINE = SEG + UTT
GROUPS = (("core",), ("z",), ("y",), ("xh",), ("xl",))
EXCHANGED = ("core", "y", "xh", "xl")


def linear(index, names, sizes):
    value = 0
    for name in names:
        value = value * sizes[name] + index[name]
    return value


def owner_pairs(sizes, flip=None):
    import itertools

    pairs = []
    for digits in itertools.product(*(range(sizes[n]) for n in FINE)):
        index = dict(zip(FINE, digits))
        source = linear(index, FINE, sizes)
        if flip is not None:
            index[flip] = sizes[flip] - 1 - index[flip]
        block = 0
        for group in GROUPS:
            size = 1
            for name in group:
                size *= sizes[name]
            block = block * size + reverse_bits(linear(index, group, sizes), size)
        pairs.append((source, block))
    return pairs


def fine_sizes(seg_size, utt_size):
    z = 8 if utt_size % 8 == 0 else utt_size
    xh = 2 if (utt_size // z) % 2 == 0 else 1
    return {"xl": seg_size // 2, "core": 2, "y": utt_size // (z * xh), "xh": xh, "z": z}


def shifted(value, axis, by):
    length = 1
    for name in axis:
        length *= lax.axis_size(name)
    pairs = [(i, i + by) for i in range(length) if 0 <= i + by < length]
    return lax.ppermute(value, axis, pairs)


def reverse_bits(value, size):
    result = 0
    bit = 1
    while bit < size:
        result = result * 2 + (value // bit) % 2
        bit *= 2
    return result


def exchange_scatter(slab, axis, dim):
    size = slab.shape[dim]
    index = reverse_bits(lax.axis_index(axis), size)
    bit = size // 2
    while bit >= 1:
        shape = slab.shape
        split = shape[:dim] + (2, shape[dim] // 2) + shape[dim + 1 :]
        halves = slab.reshape(split)
        side = (index // bit) % 2
        mine = lax.dynamic_index_in_dim(halves, side, dim, keepdims=False)
        other = lax.dynamic_index_in_dim(halves, 1 - side, dim, keepdims=False)
        flip = reverse_bits(bit, size)
        pairs = [(i, i ^ flip) for i in range(size)]
        slab = mine + lax.ppermute(other, axis, pairs)
        bit //= 2
    return slab


def round_up(value, step):
    return -(-value // step) * step


def layer_math(delayed, current, conv_one, res_one):
    channels = current.shape[1]
    paired = jnp.concatenate([delayed, current], 1)
    preact = jnp.dot(paired, conv_one, preferred_element_type=jnp.float32)
    gate_width = preact.shape[1] // 2
    gated = (jnp.tanh(preact[:, :gate_width]) * jax.nn.sigmoid(preact[:, gate_width:])).astype(
        jnp.bfloat16
    )
    following = None
    if res_one is not None:
        residual_term = jnp.dot(gated, res_one, preferred_element_type=jnp.float32)
        following = ((current.astype(jnp.float32) + residual_term) * HALF_ROOT).astype(
            jnp.bfloat16
        )
    return gated, following


def per_device(
    audio_waves, lengths, target_ids, input_weight, conv_weight, res_weight, skip_weight
):
    batch_rows, seg_len = audio_waves.shape
    layer_total = conv_weight.shape[0]
    reach = 2**layer_total - 1
    earlier = shifted(audio_waves, SEG, 1)
    window = round_up(seg_len + reach, 16)
    extended = jnp.concatenate([earlier, audio_waves], 1)[0, 2 * seg_len - window :]
    hidden = (extended[:, None] * input_weight[None, :]).astype(jnp.bfloat16)
    gated_list = []
    for layer_num in range(layer_total):
        dilation = 2**layer_num
        later_reach = 2**layer_total - 2 ** (layer_num + 1)
        in_len = hidden.shape[0]
        out_len = min(in_len, round_up(seg_len + later_reach, 16))
        if in_len - dilation >= out_len:
            delayed = hidden[in_len - out_len - dilation : in_len - dilation]
        else:
            delayed = jnp.concatenate(
                [jnp.zeros((dilation, hidden.shape[1]), hidden.dtype), hidden[: in_len - dilation]],
                0,
            )
        current = hidden[in_len - out_len :]
        res_one = res_weight[layer_num] if layer_num < layer_total - 1 else None
        gated, hidden = layer_math(delayed, current, conv_weight[layer_num], res_one)
        gated_list.append(gated[out_len - seg_len :])
    stacked = jnp.concatenate(gated_list, 1)
    skip_sum = jnp.dot(stacked, skip_weight, preferred_element_type=jnp.float32)
    features = jnp.maximum(skip_sum, 0.0).astype(jnp.bfloat16)
    skip_width = features.shape[1]
    position = lax.axis_index(SEG) * seg_len + jnp.arange(seg_len, dtype=jnp.int32)
    valid = (position[None, :] < lengths[:, None]).reshape(batch_rows * seg_len)
    masked = jnp.where(valid[:, None], features, jnp.zeros_like(features))
    frame_ids = jnp.repeat(target_ids, FRAME, axis=1).reshape(batch_rows * seg_len)
    onehot = (frame_ids[:, None] == jnp.arange(CLASSES, dtype=jnp.int32)[None, :]).astype(
        jnp.bfloat16
    )
    paired = jnp.concatenate([masked, onehot], 1)
    partial = lax.dot_general(
        masked, paired, (((0,), (0,)), ((), ())), preferred_element_type=jnp.float32
    )
    sizes = {name: lax.axis_size(name) for name in FINE}
    owners = 1
    for name in FINE:
        owners *= sizes[name]
    row_count = partial.shape[0] // owners
    width = partial.shape[1]
    group_sizes = []
    for group in GROUPS:
        size = 1
        for name in group:
            size *= sizes[name]
        group_sizes.append(size)
    local_count = jnp.sum(valid.astype(jnp.float32))
    rows = lax.broadcasted_iota(jnp.int32, partial.shape, 0)
    cols = lax.broadcasted_iota(jnp.int32, partial.shape, 1)
    slot = (rows % row_count == 1) & (cols == rows - 1)
    partial = jnp.where(slot, local_count, partial)
    pair = group_sizes[-1] * row_count
    slab = partial.reshape(tuple(group_sizes[:-1]) + (pair, width))
    slab = exchange_scatter(slab, "core", 0)
    half = width // 2
    left = exchange_scatter(slab[..., :half], "z", 1)
    right = exchange_scatter(slab[..., half:], "y", 2)
    left = exchange_scatter(left, "y", 2)
    right = exchange_scatter(right, "z", 1)
    slab = jnp.concatenate([left, right], -1)
    slab = exchange_scatter(slab, "xh", 3)
    slab = slab.reshape(tuple(slab.shape[:-2]) + (group_sizes[-1], row_count, width))
    side = lax.axis_index("xl")
    mine = lax.dynamic_index_in_dim(slab, side, 4, keepdims=True)
    other = lax.dynamic_index_in_dim(slab, 1 - side, 4, keepdims=True)
    slab = lax.ppermute(mine, FINE, owner_pairs(sizes)) + lax.ppermute(
        other, FINE, owner_pairs(sizes, flip="xl")
    )
    owned_rows = slab.reshape(row_count, width)
    first_col = lax.axis_index(FINE) * row_count
    valid_total = lax.dynamic_slice(owned_rows, (1, first_col), (1, 1))[0, 0]
    mirror = lax.dynamic_slice(owned_rows, (0, first_col + 1), (1, 1))[0, 0]
    own_rows = lax.broadcasted_iota(jnp.int32, owned_rows.shape, 0)
    own_cols = lax.broadcasted_iota(jnp.int32, owned_rows.shape, 1)
    owned_rows = jnp.where((own_rows == 1) & (own_cols == first_col), mirror, owned_rows)
    gram_rows = owned_rows[:, :skip_width] / valid_total
    cross_rows = owned_rows[:, skip_width:] * (CLASSES / valid_total)
    return (gram_rows, cross_rows)


def solution(mesh):
    sizes = fine_sizes(mesh.shape["seg"], mesh.shape["utt"])
    fine = Mesh(mesh.devices.reshape(tuple(sizes[n] for n in FINE)), FINE)
    in_specs = (P(UTT, SEG), P(UTT), P(UTT, SEG), P(), P(), P(), P())
    out_specs = (P(FINE, None), P(FINE, None))
    return jax.shard_map(
        per_device, mesh=fine, in_specs=in_specs, out_specs=out_specs, check_vma=False
    )
```

```python
import jax
import jax.numpy as jnp
from jax import lax
from jax.sharding import Mesh, PartitionSpec as P

CLASSES = 256
FRAME = 128


HALF_ROOT = 0.7071067811865476


SEG = ("xl", "core")
UTT = ("y", "xh", "z")
FINE = SEG + UTT
GROUPS = (("core",), ("z",), ("y",), ("xh",), ("xl",))
EXCHANGED = ("core", "y", "xh", "xl")


def linear(index, names, sizes):
    value = 0
    for name in names:
        value = value * sizes[name] + index[name]
    return value


def owner_pairs(sizes, flip=None):
    import itertools

    pairs = []
    for digits in itertools.product(*(range(sizes[n]) for n in FINE)):
        index = dict(zip(FINE, digits))
        source = linear(index, FINE, sizes)
        if flip is not None:
            index[flip] = sizes[flip] - 1 - index[flip]
        block = 0
        for group in GROUPS:
            size = 1
            for name in group:
                size *= sizes[name]
            block = block * size + reverse_bits(linear(index, group, sizes), size)
        pairs.append((source, block))
    return pairs


def fine_sizes(seg_size, utt_size):
    z = 8 if utt_size % 8 == 0 else utt_size
    xh = 2 if (utt_size // z) % 2 == 0 else 1
    return {"xl": seg_size // 2, "core": 2, "y": utt_size // (z * xh), "xh": xh, "z": z}


def shifted(value, axis, by):
    length = 1
    for name in axis:
        length *= lax.axis_size(name)
    pairs = [(i, i + by) for i in range(length) if 0 <= i + by < length]
    return lax.ppermute(value, axis, pairs)


def reverse_bits(value, size):
    result = 0
    bit = 1
    while bit < size:
        result = result * 2 + (value // bit) % 2
        bit *= 2
    return result


def exchange_scatter(slab, axis, dim):
    size = slab.shape[dim]
    index = reverse_bits(lax.axis_index(axis), size)
    bit = size // 2
    while bit >= 1:
        shape = slab.shape
        split = shape[:dim] + (2, shape[dim] // 2) + shape[dim + 1 :]
        halves = slab.reshape(split)
        side = (index // bit) % 2
        mine = lax.dynamic_index_in_dim(halves, side, dim, keepdims=False)
        other = lax.dynamic_index_in_dim(halves, 1 - side, dim, keepdims=False)
        flip = reverse_bits(bit, size)
        pairs = [(i, i ^ flip) for i in range(size)]
        slab = mine + lax.ppermute(other, axis, pairs)
        bit //= 2
    return slab


def round_up(value, step):
    return -(-value // step) * step


def layer_math(delayed, current, conv_one, res_one):
    channels = current.shape[1]
    paired = jnp.concatenate([delayed, current], 1)
    preact = jnp.dot(paired, conv_one, preferred_element_type=jnp.float32)
    gate_width = preact.shape[1] // 2
    gated = (jnp.tanh(preact[:, :gate_width]) * jax.nn.sigmoid(preact[:, gate_width:])).astype(
        jnp.bfloat16
    )
    following = None
    if res_one is not None:
        residual_term = jnp.dot(gated, res_one, preferred_element_type=jnp.float32)
        following = ((current.astype(jnp.float32) + residual_term) * HALF_ROOT).astype(
            jnp.bfloat16
        )
    return gated, following


def per_device(
    audio_waves, lengths, target_ids, input_weight, conv_weight, res_weight, skip_weight
):
    batch_rows, seg_len = audio_waves.shape
    layer_total = conv_weight.shape[0]
    reach = 2**layer_total - 1
    earlier = shifted(audio_waves, SEG, 1)
    window = round_up(seg_len + reach, 16)
    extended = jnp.concatenate([earlier, audio_waves], 1)[0, 2 * seg_len - window :]
    hidden = (extended[:, None] * input_weight[None, :]).astype(jnp.bfloat16)
    gated_list = []
    for layer_num in range(layer_total):
        dilation = 2**layer_num
        later_reach = 2**layer_total - 2 ** (layer_num + 1)
        in_len = hidden.shape[0]
        out_len = min(in_len, round_up(seg_len + later_reach, 16))
        if in_len - dilation >= out_len:
            delayed = hidden[in_len - out_len - dilation : in_len - dilation]
        else:
            delayed = jnp.concatenate(
                [jnp.zeros((dilation, hidden.shape[1]), hidden.dtype), hidden[: in_len - dilation]],
                0,
            )
        current = hidden[in_len - out_len :]
        res_one = res_weight[layer_num] if layer_num < layer_total - 1 else None
        gated, hidden = layer_math(delayed, current, conv_weight[layer_num], res_one)
        gated_list.append(gated[out_len - seg_len :])
    stacked = jnp.concatenate(gated_list, 1)
    skip_sum = jnp.dot(stacked, skip_weight, preferred_element_type=jnp.float32)
    features = jnp.maximum(skip_sum, 0.0).astype(jnp.bfloat16)
    skip_width = features.shape[1]
    position = lax.axis_index(SEG) * seg_len + jnp.arange(seg_len, dtype=jnp.int32)
    valid = (position[None, :] < lengths[:, None]).reshape(batch_rows * seg_len)
    masked = jnp.where(valid[:, None], features, jnp.zeros_like(features))
    frame_ids = jnp.repeat(target_ids, FRAME, axis=1).reshape(batch_rows * seg_len)
    onehot = (frame_ids[:, None] == jnp.arange(CLASSES, dtype=jnp.int32)[None, :]).astype(
        jnp.bfloat16
    )
    paired = jnp.concatenate([masked, onehot], 1)
    partial = lax.dot_general(
        masked, paired, (((0,), (0,)), ((), ())), preferred_element_type=jnp.float32
    )
    sizes = {name: lax.axis_size(name) for name in FINE}
    owners = 1
    for name in FINE:
        owners *= sizes[name]
    row_count = partial.shape[0] // owners
    width = partial.shape[1]
    group_sizes = []
    for group in GROUPS:
        size = 1
        for name in group:
            size *= sizes[name]
        group_sizes.append(size)
    local_count = jnp.sum(valid.astype(jnp.float32))
    rows = lax.broadcasted_iota(jnp.int32, partial.shape, 0)
    cols = lax.broadcasted_iota(jnp.int32, partial.shape, 1)
    slot = (rows % row_count == 1) & (cols == rows - 1)
    partial = jnp.where(slot, local_count, partial)
    pair = group_sizes[-1] * row_count
    slab = partial.reshape(tuple(group_sizes[:-1]) + (pair, width))
    slab = exchange_scatter(slab, "core", 0)
    slab = exchange_scatter(slab, "z", 1)
    slab = exchange_scatter(slab, "y", 2)
    slab = exchange_scatter(slab, "xh", 3)
    slab = slab.reshape(tuple(slab.shape[:-2]) + (group_sizes[-1], row_count, width))
    side = lax.axis_index("xl")
    mine = lax.dynamic_index_in_dim(slab, side, 4, keepdims=True)
    other = lax.dynamic_index_in_dim(slab, 1 - side, 4, keepdims=True)
    slab = lax.ppermute(mine, FINE, owner_pairs(sizes)) + lax.ppermute(
        other, FINE, owner_pairs(sizes, flip="xl")
    )
    owned_rows = slab.reshape(row_count, width)
    first_col = lax.axis_index(FINE) * row_count
    valid_total = lax.dynamic_slice(owned_rows, (1, first_col), (1, 1))[0, 0]
    mirror = lax.dynamic_slice(owned_rows, (0, first_col + 1), (1, 1))[0, 0]
    own_rows = lax.broadcasted_iota(jnp.int32, owned_rows.shape, 0)
    own_cols = lax.broadcasted_iota(jnp.int32, owned_rows.shape, 1)
    owned_rows = jnp.where((own_rows == 1) & (own_cols == first_col), mirror, owned_rows)
    gram_rows = owned_rows[:, :skip_width] / valid_total
    cross_rows = owned_rows[:, skip_width:] * (CLASSES / valid_total)
    return (gram_rows, cross_rows)


def solution(mesh):
    sizes = fine_sizes(mesh.shape["seg"], mesh.shape["utt"])
    fine = Mesh(mesh.devices.reshape(tuple(sizes[n] for n in FINE)), FINE)
    in_specs = (P(UTT, SEG), P(UTT), P(UTT, SEG), P(), P(), P(), P())
    out_specs = (P(FINE, None), P(FINE, None))
    return jax.shard_map(
        per_device, mesh=fine, in_specs=in_specs, out_specs=out_specs, check_vma=False
    )
```

```python
import jax
import jax.numpy as jnp
from jax import lax
from jax.sharding import Mesh, PartitionSpec as P

CLASSES = 256
FRAME = 128


HALF_ROOT = 0.7071067811865476


SEG = ("xl", "core")
UTT = ("y", "xh", "z")
FINE = SEG + UTT
GROUPS = (("core",), ("z",), ("y",), ("xh",), ("xl",))
EXCHANGED = ("core", "y", "xh", "xl")


def linear(index, names, sizes):
    value = 0
    for name in names:
        value = value * sizes[name] + index[name]
    return value


def owner_pairs(sizes, flip=None):
    import itertools

    pairs = []
    for digits in itertools.product(*(range(sizes[n]) for n in FINE)):
        index = dict(zip(FINE, digits))
        source = linear(index, FINE, sizes)
        if flip is not None:
            index[flip] = sizes[flip] - 1 - index[flip]
        block = 0
        for group in GROUPS:
            size = 1
            for name in group:
                size *= sizes[name]
            block = block * size + reverse_bits(linear(index, group, sizes), size)
        pairs.append((source, block))
    return pairs


def fine_sizes(seg_size, utt_size):
    z = 8 if utt_size % 8 == 0 else utt_size
    xh = 2 if (utt_size // z) % 2 == 0 else 1
    return {"xl": seg_size // 2, "core": 2, "y": utt_size // (z * xh), "xh": xh, "z": z}


def shifted(value, axis, by):
    length = 1
    for name in axis:
        length *= lax.axis_size(name)
    pairs = [(i, i + by) for i in range(length) if 0 <= i + by < length]
    return lax.ppermute(value, axis, pairs)


def reverse_bits(value, size):
    result = 0
    bit = 1
    while bit < size:
        result = result * 2 + (value // bit) % 2
        bit *= 2
    return result


def exchange_scatter(slab, axis, dim):
    size = slab.shape[dim]
    index = reverse_bits(lax.axis_index(axis), size)
    bit = size // 2
    while bit >= 1:
        shape = slab.shape
        split = shape[:dim] + (2, shape[dim] // 2) + shape[dim + 1 :]
        halves = slab.reshape(split)
        side = (index // bit) % 2
        mine = lax.dynamic_index_in_dim(halves, side, dim, keepdims=False)
        other = lax.dynamic_index_in_dim(halves, 1 - side, dim, keepdims=False)
        flip = reverse_bits(bit, size)
        pairs = [(i, i ^ flip) for i in range(size)]
        slab = mine + lax.ppermute(other, axis, pairs)
        bit //= 2
    return slab


def round_up(value, step):
    return -(-value // step) * step


def layer_math(delayed, current, conv_one, res_one):
    channels = current.shape[1]
    paired = jnp.concatenate([delayed, current], 1)
    preact = jnp.dot(paired, conv_one, preferred_element_type=jnp.float32)
    gate_width = preact.shape[1] // 2
    gated = (jnp.tanh(preact[:, :gate_width]) * jax.nn.sigmoid(preact[:, gate_width:])).astype(
        jnp.bfloat16
    )
    following = None
    if res_one is not None:
        residual_term = jnp.dot(gated, res_one, preferred_element_type=jnp.float32)
        following = ((current.astype(jnp.float32) + residual_term) * HALF_ROOT).astype(
            jnp.bfloat16
        )
    return gated, following


def per_device(
    audio_waves, lengths, target_ids, input_weight, conv_weight, res_weight, skip_weight
):
    batch_rows, seg_len = audio_waves.shape
    layer_total = conv_weight.shape[0]
    reach = 2**layer_total - 1
    earlier = shifted(audio_waves, SEG, 1)
    window = round_up(seg_len + reach, 16)
    extended = jnp.concatenate([earlier, audio_waves], 1)[0, 2 * seg_len - window :]
    hidden = (extended[:, None] * input_weight[None, :]).astype(jnp.bfloat16)
    gated_list = []
    for layer_num in range(layer_total):
        dilation = 2**layer_num
        later_reach = 2**layer_total - 2 ** (layer_num + 1)
        in_len = hidden.shape[0]
        out_len = min(in_len, round_up(seg_len + later_reach, 16))
        if in_len - dilation >= out_len:
            delayed = hidden[in_len - out_len - dilation : in_len - dilation]
        else:
            delayed = jnp.concatenate(
                [jnp.zeros((dilation, hidden.shape[1]), hidden.dtype), hidden[: in_len - dilation]],
                0,
            )
        current = hidden[in_len - out_len :]
        res_one = res_weight[layer_num] if layer_num < layer_total - 1 else None
        gated, hidden = layer_math(delayed, current, conv_weight[layer_num], res_one)
        gated_list.append(gated[out_len - seg_len :])
    stacked = jnp.concatenate(gated_list, 1)
    skip_sum = jnp.dot(stacked, skip_weight, preferred_element_type=jnp.float32)
    features = jnp.maximum(skip_sum, 0.0).astype(jnp.bfloat16)
    skip_width = features.shape[1]
    position = lax.axis_index(SEG) * seg_len + jnp.arange(seg_len, dtype=jnp.int32)
    valid = (position[None, :] < lengths[:, None]).reshape(batch_rows * seg_len)
    masked = jnp.where(valid[:, None], features, jnp.zeros_like(features))
    frame_ids = jnp.repeat(target_ids, FRAME, axis=1).reshape(batch_rows * seg_len)
    onehot = (frame_ids[:, None] == jnp.arange(CLASSES, dtype=jnp.int32)[None, :]).astype(
        jnp.bfloat16
    )
    paired = jnp.concatenate([masked, onehot], 1)
    partial = lax.dot_general(
        masked, paired, (((0,), (0,)), ((), ())), preferred_element_type=jnp.float32
    )
    sizes = {name: lax.axis_size(name) for name in FINE}
    owners = 1
    for name in FINE:
        owners *= sizes[name]
    row_count = partial.shape[0] // owners
    width = partial.shape[1]
    group_sizes = []
    for group in GROUPS:
        size = 1
        for name in group:
            size *= sizes[name]
        group_sizes.append(size)
    local_count = jnp.sum(valid.astype(jnp.float32))
    rows = lax.broadcasted_iota(jnp.int32, partial.shape, 0)
    cols = lax.broadcasted_iota(jnp.int32, partial.shape, 1)
    slot = (rows % row_count == 1) & (cols == rows - 1)
    partial = jnp.where(slot, local_count, partial)
    pair = group_sizes[-1] * row_count
    slab = partial.reshape(tuple(group_sizes[:-1]) + (pair, width))
    slab = exchange_scatter(slab, "core", 0)
    first = (width // 128 * 2 // 5) * 128
    second = first + (width - first) // 256 * 128
    part_a = slab[..., :first]
    part_b = slab[..., first:second]
    part_c = slab[..., second:]
    part_a = exchange_scatter(part_a, "z", 1)
    part_b = exchange_scatter(part_b, "y", 2)
    part_c = exchange_scatter(part_c, "xh", 3)
    part_a = exchange_scatter(part_a, "y", 2)
    part_b = exchange_scatter(part_b, "z", 1)
    part_c = exchange_scatter(part_c, "z", 1)
    part_a = exchange_scatter(part_a, "xh", 3)
    part_b = exchange_scatter(part_b, "xh", 3)
    part_c = exchange_scatter(part_c, "y", 2)
    slab = jnp.concatenate([part_a, part_b, part_c], -1)
    slab = slab.reshape(tuple(slab.shape[:-2]) + (group_sizes[-1], row_count, width))
    side = lax.axis_index("xl")
    mine = lax.dynamic_index_in_dim(slab, side, 4, keepdims=True)
    other = lax.dynamic_index_in_dim(slab, 1 - side, 4, keepdims=True)
    slab = lax.ppermute(mine, FINE, owner_pairs(sizes)) + lax.ppermute(
        other, FINE, owner_pairs(sizes, flip="xl")
    )
    owned_rows = slab.reshape(row_count, width)
    first_col = lax.axis_index(FINE) * row_count
    valid_total = lax.dynamic_slice(owned_rows, (1, first_col), (1, 1))[0, 0]
    mirror = lax.dynamic_slice(owned_rows, (0, first_col + 1), (1, 1))[0, 0]
    own_rows = lax.broadcasted_iota(jnp.int32, owned_rows.shape, 0)
    own_cols = lax.broadcasted_iota(jnp.int32, owned_rows.shape, 1)
    owned_rows = jnp.where((own_rows == 1) & (own_cols == first_col), mirror, owned_rows)
    gram_rows = owned_rows[:, :skip_width] / valid_total
    cross_rows = owned_rows[:, skip_width:] * (CLASSES / valid_total)
    return (gram_rows, cross_rows)


def solution(mesh):
    sizes = fine_sizes(mesh.shape["seg"], mesh.shape["utt"])
    fine = Mesh(mesh.devices.reshape(tuple(sizes[n] for n in FINE)), FINE)
    in_specs = (P(UTT, SEG), P(UTT), P(UTT, SEG), P(), P(), P(), P())
    out_specs = (P(FINE, None), P(FINE, None))
    return jax.shard_map(
        per_device, mesh=fine, in_specs=in_specs, out_specs=out_specs, check_vma=False
    )
```

```python
import jax
import jax.numpy as jnp
from jax import lax
from jax.sharding import Mesh, PartitionSpec as P

CLASSES = 256
FRAME = 128


HALF_ROOT = 0.7071067811865476


SEG = ("xl", "core")
UTT = ("y", "xh", "z")
FINE = SEG + UTT
GROUPS = (("core",), ("z",), ("y",), ("xh",), ("xl",))
EXCHANGED = ("core", "y", "xh", "xl")


def linear(index, names, sizes):
    value = 0
    for name in names:
        value = value * sizes[name] + index[name]
    return value


def owner_pairs(sizes):
    import itertools

    pairs = []
    for digits in itertools.product(*(range(sizes[n]) for n in FINE)):
        index = dict(zip(FINE, digits))
        block = 0
        for group in GROUPS:
            size = 1
            for name in group:
                size *= sizes[name]
            block = block * size + reverse_bits(linear(index, group, sizes), size)
        pairs.append((linear(index, FINE, sizes), block))
    return pairs


def fine_sizes(seg_size, utt_size):
    z = 8 if utt_size % 8 == 0 else utt_size
    xh = 2 if (utt_size // z) % 2 == 0 else 1
    return {"xl": seg_size // 2, "core": 2, "y": utt_size // (z * xh), "xh": xh, "z": z}


def shifted(value, axis, by):
    length = 1
    for name in axis:
        length *= lax.axis_size(name)
    pairs = [(i, i + by) for i in range(length) if 0 <= i + by < length]
    return lax.ppermute(value, axis, pairs)


def reverse_bits(value, size):
    result = 0
    bit = 1
    while bit < size:
        result = result * 2 + (value // bit) % 2
        bit *= 2
    return result


def exchange_scatter(slab, axis, dim):
    size = slab.shape[dim]
    index = reverse_bits(lax.axis_index(axis), size)
    bit = size // 2
    while bit >= 1:
        shape = slab.shape
        split = shape[:dim] + (2, shape[dim] // 2) + shape[dim + 1 :]
        halves = slab.reshape(split)
        side = (index // bit) % 2
        mine = lax.dynamic_index_in_dim(halves, side, dim, keepdims=False)
        other = lax.dynamic_index_in_dim(halves, 1 - side, dim, keepdims=False)
        flip = reverse_bits(bit, size)
        pairs = [(i, i ^ flip) for i in range(size)]
        slab = mine + lax.ppermute(other, axis, pairs)
        bit //= 2
    return slab


def round_up(value, step):
    return -(-value // step) * step


def layer_math(delayed, current, conv_one, res_one):
    channels = current.shape[1]
    paired = jnp.concatenate([delayed, current], 1)
    preact = jnp.dot(paired, conv_one, preferred_element_type=jnp.float32)
    gate_width = preact.shape[1] // 2
    gated = (jnp.tanh(preact[:, :gate_width]) * jax.nn.sigmoid(preact[:, gate_width:])).astype(
        jnp.bfloat16
    )
    following = None
    if res_one is not None:
        residual_term = jnp.dot(gated, res_one, preferred_element_type=jnp.float32)
        following = ((current.astype(jnp.float32) + residual_term) * HALF_ROOT).astype(
            jnp.bfloat16
        )
    return gated, following


def per_device(
    audio_waves, lengths, target_ids, input_weight, conv_weight, res_weight, skip_weight
):
    batch_rows, seg_len = audio_waves.shape
    layer_total = conv_weight.shape[0]
    reach = 2**layer_total - 1
    earlier = shifted(audio_waves, SEG, 1)
    window = round_up(seg_len + reach, 16)
    extended = jnp.concatenate([earlier, audio_waves], 1)[0, 2 * seg_len - window :]
    hidden = (extended[:, None] * input_weight[None, :]).astype(jnp.bfloat16)
    gated_list = []
    for layer_num in range(layer_total):
        dilation = 2**layer_num
        later_reach = 2**layer_total - 2 ** (layer_num + 1)
        in_len = hidden.shape[0]
        out_len = min(in_len, round_up(seg_len + later_reach, 16))
        if in_len - dilation >= out_len:
            delayed = hidden[in_len - out_len - dilation : in_len - dilation]
        else:
            delayed = jnp.concatenate(
                [jnp.zeros((dilation, hidden.shape[1]), hidden.dtype), hidden[: in_len - dilation]],
                0,
            )
        current = hidden[in_len - out_len :]
        res_one = res_weight[layer_num] if layer_num < layer_total - 1 else None
        gated, hidden = layer_math(delayed, current, conv_weight[layer_num], res_one)
        gated_list.append(gated[out_len - seg_len :])
    stacked = jnp.concatenate(gated_list, 1)
    skip_sum = jnp.dot(stacked, skip_weight, preferred_element_type=jnp.float32)
    features = jnp.maximum(skip_sum, 0.0).astype(jnp.bfloat16)
    skip_width = features.shape[1]
    position = lax.axis_index(SEG) * seg_len + jnp.arange(seg_len, dtype=jnp.int32)
    valid = (position[None, :] < lengths[:, None]).reshape(batch_rows * seg_len)
    masked = jnp.where(valid[:, None], features, jnp.zeros_like(features))
    frame_ids = jnp.repeat(target_ids, FRAME, axis=1).reshape(batch_rows * seg_len)
    onehot = (frame_ids[:, None] == jnp.arange(CLASSES, dtype=jnp.int32)[None, :]).astype(
        jnp.bfloat16
    )
    paired = jnp.concatenate([masked, onehot], 1)
    sizes = {name: lax.axis_size(name) for name in FINE}
    owners = 1
    for name in FINE:
        owners *= sizes[name]
    row_count = skip_width // owners
    width = paired.shape[1]
    group_sizes = []
    for group in GROUPS:
        size = 1
        for name in group:
            size *= sizes[name]
        group_sizes.append(size)
    pair = group_sizes[-1] * row_count
    local_count = jnp.sum(valid.astype(jnp.float32))
    cores = group_sizes[0]
    core_rows = skip_width // cores
    core = lax.axis_index("core")

    def core_half(part):
        lhs = lax.dynamic_slice_in_dim(masked, part * core_rows, core_rows, 1)
        rows_part = lax.dot_general(
            lhs, paired, (((0,), (0,)), ((), ())), preferred_element_type=jnp.float32
        )
        rows = lax.broadcasted_iota(jnp.int32, rows_part.shape, 0) + part * core_rows
        cols = lax.broadcasted_iota(jnp.int32, rows_part.shape, 1)
        slot = (rows % row_count == 1) & (cols == rows - 1)
        rows_part = jnp.where(slot, local_count, rows_part)
        return rows_part.reshape((1,) + tuple(group_sizes[1:-1]) + (pair, width))

    sent = lax.ppermute(core_half(1 - core), "core", [(i, i ^ 1) for i in range(cores)])
    slab = core_half(core) + sent
    half = width // 2
    left = exchange_scatter(slab[..., :half], "z", 1)
    right = exchange_scatter(slab[..., half:], "y", 2)
    left = exchange_scatter(left, "y", 2)
    right = exchange_scatter(right, "z", 1)
    slab = jnp.concatenate([left, right], -1)
    slab = exchange_scatter(slab, "xh", 3)
    slab = slab.reshape(tuple(slab.shape[:-2]) + (group_sizes[-1], row_count, width))
    slab = exchange_scatter(slab, "xl", 4)
    slab = lax.ppermute(slab, FINE, owner_pairs(sizes))
    owned_rows = slab.reshape(row_count, width)
    first_col = lax.axis_index(FINE) * row_count
    valid_total = lax.dynamic_slice(owned_rows, (1, first_col), (1, 1))[0, 0]
    mirror = lax.dynamic_slice(owned_rows, (0, first_col + 1), (1, 1))[0, 0]
    own_rows = lax.broadcasted_iota(jnp.int32, owned_rows.shape, 0)
    own_cols = lax.broadcasted_iota(jnp.int32, owned_rows.shape, 1)
    owned_rows = jnp.where((own_rows == 1) & (own_cols == first_col), mirror, owned_rows)
    gram_rows = owned_rows[:, :skip_width] / valid_total
    cross_rows = owned_rows[:, skip_width:] * (CLASSES / valid_total)
    return (gram_rows, cross_rows)


def solution(mesh):
    sizes = fine_sizes(mesh.shape["seg"], mesh.shape["utt"])
    fine = Mesh(mesh.devices.reshape(tuple(sizes[n] for n in FINE)), FINE)
    in_specs = (P(UTT, SEG), P(UTT), P(UTT, SEG), P(), P(), P(), P())
    out_specs = (P(FINE, None), P(FINE, None))
    return jax.shard_map(
        per_device, mesh=fine, in_specs=in_specs, out_specs=out_specs, check_vma=False
    )
```

```python
import jax
import jax.numpy as jnp
from jax import lax
from jax.sharding import Mesh, PartitionSpec as P

CLASSES = 256
FRAME = 128


HALF_ROOT = 0.7071067811865476


SEG = ("xl", "core")
UTT = ("y", "xh", "z")
FINE = SEG + UTT
GROUPS = (("core",), ("z",), ("y",), ("xh",), ("xl",))
EXCHANGED = ("core", "y", "xh", "xl")


def linear(index, names, sizes):
    value = 0
    for name in names:
        value = value * sizes[name] + index[name]
    return value


def owner_pairs(sizes):
    import itertools

    pairs = []
    for digits in itertools.product(*(range(sizes[n]) for n in FINE)):
        index = dict(zip(FINE, digits))
        block = 0
        for group in GROUPS:
            size = 1
            for name in group:
                size *= sizes[name]
            block = block * size + reverse_bits(linear(index, group, sizes), size)
        pairs.append((linear(index, FINE, sizes), block))
    return pairs


def fine_sizes(seg_size, utt_size):
    z = 8 if utt_size % 8 == 0 else utt_size
    xh = 2 if (utt_size // z) % 2 == 0 else 1
    return {"xl": seg_size // 2, "core": 2, "y": utt_size // (z * xh), "xh": xh, "z": z}


def shifted(value, axis, by):
    length = 1
    for name in axis:
        length *= lax.axis_size(name)
    pairs = [(i, i + by) for i in range(length) if 0 <= i + by < length]
    return lax.ppermute(value, axis, pairs)


def reverse_bits(value, size):
    result = 0
    bit = 1
    while bit < size:
        result = result * 2 + (value // bit) % 2
        bit *= 2
    return result


def exchange_scatter(slab, axis, dim):
    size = slab.shape[dim]
    index = reverse_bits(lax.axis_index(axis), size)
    bit = size // 2
    while bit >= 1:
        shape = slab.shape
        split = shape[:dim] + (2, shape[dim] // 2) + shape[dim + 1 :]
        halves = slab.reshape(split)
        side = (index // bit) % 2
        mine = lax.dynamic_index_in_dim(halves, side, dim, keepdims=False)
        other = lax.dynamic_index_in_dim(halves, 1 - side, dim, keepdims=False)
        flip = reverse_bits(bit, size)
        pairs = [(i, i ^ flip) for i in range(size)]
        slab = mine + lax.ppermute(other, axis, pairs)
        bit //= 2
    return slab


def round_up(value, step):
    return -(-value // step) * step


def layer_math(delayed, current, conv_one, res_one):
    channels = current.shape[1]
    paired = jnp.concatenate([delayed, current], 1)
    preact = jnp.dot(paired, conv_one, preferred_element_type=jnp.float32)
    gate_width = preact.shape[1] // 2
    gated = (jnp.tanh(preact[:, :gate_width]) * jax.nn.sigmoid(preact[:, gate_width:])).astype(
        jnp.bfloat16
    )
    following = None
    if res_one is not None:
        residual_term = jnp.dot(gated, res_one, preferred_element_type=jnp.float32)
        following = ((current.astype(jnp.float32) + residual_term) * HALF_ROOT).astype(
            jnp.bfloat16
        )
    return gated, following


def per_device(
    audio_waves, lengths, target_ids, input_weight, conv_weight, res_weight, skip_weight
):
    batch_rows, seg_len = audio_waves.shape
    layer_total = conv_weight.shape[0]
    reach = 2**layer_total - 1
    earlier = shifted(audio_waves, SEG, 1)
    window = round_up(seg_len + reach, 16)
    extended = jnp.concatenate([earlier, audio_waves], 1)[0, 2 * seg_len - window :]
    hidden = (extended[:, None] * input_weight[None, :]).astype(jnp.bfloat16)
    gated_list = []
    for layer_num in range(layer_total):
        dilation = 2**layer_num
        later_reach = 2**layer_total - 2 ** (layer_num + 1)
        in_len = hidden.shape[0]
        out_len = min(in_len, round_up(seg_len + later_reach, 16))
        if in_len - dilation >= out_len:
            delayed = hidden[in_len - out_len - dilation : in_len - dilation]
        else:
            delayed = jnp.concatenate(
                [jnp.zeros((dilation, hidden.shape[1]), hidden.dtype), hidden[: in_len - dilation]],
                0,
            )
        current = hidden[in_len - out_len :]
        res_one = res_weight[layer_num] if layer_num < layer_total - 1 else None
        gated, hidden = layer_math(delayed, current, conv_weight[layer_num], res_one)
        gated_list.append(gated[out_len - seg_len :])
    stacked = jnp.concatenate(gated_list, 1)
    skip_sum = jnp.dot(stacked, skip_weight, preferred_element_type=jnp.float32)
    features = jnp.maximum(skip_sum, 0.0).astype(jnp.bfloat16)
    skip_width = features.shape[1]
    position = lax.axis_index(SEG) * seg_len + jnp.arange(seg_len, dtype=jnp.int32)
    valid = (position[None, :] < lengths[:, None]).reshape(batch_rows * seg_len)
    masked = jnp.where(valid[:, None], features, jnp.zeros_like(features))
    frame_ids = jnp.repeat(target_ids, FRAME, axis=1).reshape(batch_rows * seg_len)
    onehot = (frame_ids[:, None] == jnp.arange(CLASSES, dtype=jnp.int32)[None, :]).astype(
        jnp.bfloat16
    )
    paired = jnp.concatenate([masked, onehot], 1)
    sizes = {name: lax.axis_size(name) for name in FINE}
    owners = 1
    for name in FINE:
        owners *= sizes[name]
    row_count = skip_width // owners
    width = paired.shape[1]
    group_sizes = []
    for group in GROUPS:
        size = 1
        for name in group:
            size *= sizes[name]
        group_sizes.append(size)
    pair = group_sizes[-1] * row_count
    local_count = jnp.sum(valid.astype(jnp.float32))
    cores = group_sizes[0]
    core_rows = skip_width // cores
    core = lax.axis_index("core")

    half = width // 2

    def core_half(part, first_col):
        lhs = lax.dynamic_slice_in_dim(masked, part * core_rows, core_rows, 1)
        rhs = paired[:, first_col : first_col + half]
        rows_part = lax.dot_general(
            lhs, rhs, (((0,), (0,)), ((), ())), preferred_element_type=jnp.float32
        )
        rows = lax.broadcasted_iota(jnp.int32, rows_part.shape, 0) + part * core_rows
        cols = lax.broadcasted_iota(jnp.int32, rows_part.shape, 1) + first_col
        slot = (rows % row_count == 1) & (cols == rows - 1)
        rows_part = jnp.where(slot, local_count, rows_part)
        return rows_part.reshape((1,) + tuple(group_sizes[1:-1]) + (pair, half))

    partner = [(i, i ^ 1) for i in range(cores)]
    sent_left = lax.ppermute(core_half(1 - core, 0), "core", partner)
    sent_right = lax.ppermute(core_half(1 - core, half), "core", partner)
    left_slab = core_half(core, 0) + sent_left
    right_slab = core_half(core, half) + sent_right
    left = exchange_scatter(left_slab, "z", 1)
    right = exchange_scatter(right_slab, "y", 2)
    left = exchange_scatter(left, "y", 2)
    right = exchange_scatter(right, "z", 1)
    slab = jnp.concatenate([left, right], -1)
    slab = exchange_scatter(slab, "xh", 3)
    slab = slab.reshape(tuple(slab.shape[:-2]) + (group_sizes[-1], row_count, width))
    slab = exchange_scatter(slab, "xl", 4)
    slab = lax.ppermute(slab, FINE, owner_pairs(sizes))
    owned_rows = slab.reshape(row_count, width)
    first_col = lax.axis_index(FINE) * row_count
    valid_total = lax.dynamic_slice(owned_rows, (1, first_col), (1, 1))[0, 0]
    mirror = lax.dynamic_slice(owned_rows, (0, first_col + 1), (1, 1))[0, 0]
    own_rows = lax.broadcasted_iota(jnp.int32, owned_rows.shape, 0)
    own_cols = lax.broadcasted_iota(jnp.int32, owned_rows.shape, 1)
    owned_rows = jnp.where((own_rows == 1) & (own_cols == first_col), mirror, owned_rows)
    gram_rows = owned_rows[:, :skip_width] / valid_total
    cross_rows = owned_rows[:, skip_width:] * (CLASSES / valid_total)
    return (gram_rows, cross_rows)


def solution(mesh):
    sizes = fine_sizes(mesh.shape["seg"], mesh.shape["utt"])
    fine = Mesh(mesh.devices.reshape(tuple(sizes[n] for n in FINE)), FINE)
    in_specs = (P(UTT, SEG), P(UTT), P(UTT, SEG), P(), P(), P(), P())
    out_specs = (P(FINE, None), P(FINE, None))
    return jax.shard_map(
        per_device, mesh=fine, in_specs=in_specs, out_specs=out_specs, check_vma=False
    )
```

```python
import jax
import jax.numpy as jnp
from jax import lax
from jax.sharding import Mesh, PartitionSpec as P

CLASSES = 256
FRAME = 128


HALF_ROOT = 0.7071067811865476


SEG = ("xl", "core")
UTT = ("y", "xh", "z")
FINE = SEG + UTT
GROUPS = (("core",), ("z",), ("y",), ("xh",), ("xl",))
EXCHANGED = ("core", "y", "xh", "xl")


def linear(index, names, sizes):
    value = 0
    for name in names:
        value = value * sizes[name] + index[name]
    return value


def owner_pairs(sizes):
    import itertools

    pairs = []
    for digits in itertools.product(*(range(sizes[n]) for n in FINE)):
        index = dict(zip(FINE, digits))
        block = 0
        for group in GROUPS:
            size = 1
            for name in group:
                size *= sizes[name]
            block = block * size + reverse_bits(linear(index, group, sizes), size)
        pairs.append((linear(index, FINE, sizes), block))
    return pairs


def fine_sizes(seg_size, utt_size):
    z = 8 if utt_size % 8 == 0 else utt_size
    xh = 2 if (utt_size // z) % 2 == 0 else 1
    return {"xl": seg_size // 2, "core": 2, "y": utt_size // (z * xh), "xh": xh, "z": z}


def shifted(value, axis, by):
    length = 1
    for name in axis:
        length *= lax.axis_size(name)
    pairs = [(i, i + by) for i in range(length) if 0 <= i + by < length]
    return lax.ppermute(value, axis, pairs)


def reverse_bits(value, size):
    result = 0
    bit = 1
    while bit < size:
        result = result * 2 + (value // bit) % 2
        bit *= 2
    return result


def exchange_scatter(slab, axis, dim):
    size = slab.shape[dim]
    index = reverse_bits(lax.axis_index(axis), size)
    bit = size // 2
    while bit >= 1:
        shape = slab.shape
        split = shape[:dim] + (2, shape[dim] // 2) + shape[dim + 1 :]
        halves = slab.reshape(split)
        side = (index // bit) % 2
        mine = lax.dynamic_index_in_dim(halves, side, dim, keepdims=False)
        other = lax.dynamic_index_in_dim(halves, 1 - side, dim, keepdims=False)
        flip = reverse_bits(bit, size)
        pairs = [(i, i ^ flip) for i in range(size)]
        slab = mine + lax.ppermute(other, axis, pairs)
        bit //= 2
    return slab


def round_up(value, step):
    return -(-value // step) * step


def layer_math(delayed, current, conv_one, res_one):
    channels = current.shape[1]
    paired = jnp.concatenate([delayed, current], 1)
    preact = jnp.dot(paired, conv_one, preferred_element_type=jnp.float32)
    gate_width = preact.shape[1] // 2
    gated = (jnp.tanh(preact[:, :gate_width]) * jax.nn.sigmoid(preact[:, gate_width:])).astype(
        jnp.bfloat16
    )
    following = None
    if res_one is not None:
        residual_term = jnp.dot(gated, res_one, preferred_element_type=jnp.float32)
        following = ((current.astype(jnp.float32) + residual_term) * HALF_ROOT).astype(
            jnp.bfloat16
        )
    return gated, following


def per_device(
    audio_waves, lengths, target_ids, input_weight, conv_weight, res_weight, skip_weight
):
    batch_rows, seg_len = audio_waves.shape
    layer_total = conv_weight.shape[0]
    reach = 2**layer_total - 1
    earlier = shifted(audio_waves, SEG, 1)
    window = round_up(seg_len + reach, 16)
    extended = jnp.concatenate([earlier, audio_waves], 1)[0, 2 * seg_len - window :]
    hidden = (extended[:, None] * input_weight[None, :]).astype(jnp.bfloat16)
    gated_list = []
    for layer_num in range(layer_total):
        dilation = 2**layer_num
        later_reach = 2**layer_total - 2 ** (layer_num + 1)
        in_len = hidden.shape[0]
        out_len = min(in_len, round_up(seg_len + later_reach, 16))
        if in_len - dilation >= out_len:
            delayed = hidden[in_len - out_len - dilation : in_len - dilation]
        else:
            delayed = jnp.concatenate(
                [jnp.zeros((dilation, hidden.shape[1]), hidden.dtype), hidden[: in_len - dilation]],
                0,
            )
        current = hidden[in_len - out_len :]
        res_one = res_weight[layer_num] if layer_num < layer_total - 1 else None
        gated, hidden = layer_math(delayed, current, conv_weight[layer_num], res_one)
        gated_list.append(gated[out_len - seg_len :])
    stacked = jnp.concatenate(gated_list, 1)
    skip_sum = jnp.dot(stacked, skip_weight, preferred_element_type=jnp.float32)
    features = jnp.maximum(skip_sum, 0.0).astype(jnp.bfloat16)
    skip_width = features.shape[1]
    position = lax.axis_index(SEG) * seg_len + jnp.arange(seg_len, dtype=jnp.int32)
    valid = (position[None, :] < lengths[:, None]).reshape(batch_rows * seg_len)
    masked = jnp.where(valid[:, None], features, jnp.zeros_like(features))
    frame_ids = jnp.repeat(target_ids, FRAME, axis=1).reshape(batch_rows * seg_len)
    onehot = (frame_ids[:, None] == jnp.arange(CLASSES, dtype=jnp.int32)[None, :]).astype(
        jnp.bfloat16
    )
    paired = jnp.concatenate([masked, onehot], 1)
    sizes = {name: lax.axis_size(name) for name in FINE}
    owners = 1
    for name in FINE:
        owners *= sizes[name]
    row_count = skip_width // owners
    width = paired.shape[1]
    group_sizes = []
    for group in GROUPS:
        size = 1
        for name in group:
            size *= sizes[name]
        group_sizes.append(size)
    pair = group_sizes[-1] * row_count
    local_count = jnp.sum(valid.astype(jnp.float32))
    cores = group_sizes[0]
    core_rows = skip_width // cores
    core = lax.axis_index("core")

    def core_half(part):
        lhs = lax.dynamic_slice_in_dim(masked, part * core_rows, core_rows, 1)
        rows_part = lax.dot_general(
            lhs, paired, (((0,), (0,)), ((), ())), preferred_element_type=jnp.float32
        )
        rows = lax.broadcasted_iota(jnp.int32, rows_part.shape, 0) + part * core_rows
        cols = lax.broadcasted_iota(jnp.int32, rows_part.shape, 1)
        slot = (rows % row_count == 1) & (cols == rows - 1)
        rows_part = jnp.where(slot, local_count, rows_part)
        return rows_part.reshape((1,) + tuple(group_sizes[1:-1]) + (pair, width))

    sent = lax.ppermute(core_half(1 - core), "core", [(i, i ^ 1) for i in range(cores)])
    slab = core_half(core) + sent
    half = (width // 128 * 2 // 5) * 128
    left = exchange_scatter(slab[..., :half], "z", 1)
    right = exchange_scatter(slab[..., half:], "y", 2)
    left = exchange_scatter(left, "y", 2)
    right = exchange_scatter(right, "z", 1)
    slab = jnp.concatenate([left, right], -1)
    slab = exchange_scatter(slab, "xh", 3)
    slab = slab.reshape(tuple(slab.shape[:-2]) + (group_sizes[-1], row_count, width))
    slab = exchange_scatter(slab, "xl", 4)
    slab = lax.ppermute(slab, FINE, owner_pairs(sizes))
    owned_rows = slab.reshape(row_count, width)
    first_col = lax.axis_index(FINE) * row_count
    valid_total = lax.dynamic_slice(owned_rows, (1, first_col), (1, 1))[0, 0]
    mirror = lax.dynamic_slice(owned_rows, (0, first_col + 1), (1, 1))[0, 0]
    own_rows = lax.broadcasted_iota(jnp.int32, owned_rows.shape, 0)
    own_cols = lax.broadcasted_iota(jnp.int32, owned_rows.shape, 1)
    owned_rows = jnp.where((own_rows == 1) & (own_cols == first_col), mirror, owned_rows)
    gram_rows = owned_rows[:, :skip_width] / valid_total
    cross_rows = owned_rows[:, skip_width:] * (CLASSES / valid_total)
    return (gram_rows, cross_rows)


def solution(mesh):
    sizes = fine_sizes(mesh.shape["seg"], mesh.shape["utt"])
    fine = Mesh(mesh.devices.reshape(tuple(sizes[n] for n in FINE)), FINE)
    in_specs = (P(UTT, SEG), P(UTT), P(UTT, SEG), P(), P(), P(), P())
    out_specs = (P(FINE, None), P(FINE, None))
    return jax.shard_map(
        per_device, mesh=fine, in_specs=in_specs, out_specs=out_specs, check_vma=False
    )
```

```python
import jax
import jax.numpy as jnp
from jax import lax
from jax.sharding import Mesh, PartitionSpec as P

CLASSES = 256
FRAME = 128


HALF_ROOT = 0.7071067811865476


SEG = ("xl", "core")
UTT = ("y", "xh", "z")
FINE = SEG + UTT
GROUPS = (("core",), ("z",), ("y",), ("xh",), ("xl",))
EXCHANGED = ("core", "y", "xh", "xl")


def linear(index, names, sizes):
    value = 0
    for name in names:
        value = value * sizes[name] + index[name]
    return value


def owner_pairs(sizes):
    import itertools

    pairs = []
    for digits in itertools.product(*(range(sizes[n]) for n in FINE)):
        index = dict(zip(FINE, digits))
        block = 0
        for group in GROUPS:
            size = 1
            for name in group:
                size *= sizes[name]
            block = block * size + reverse_bits(linear(index, group, sizes), size)
        pairs.append((linear(index, FINE, sizes), block))
    return pairs


def fine_sizes(seg_size, utt_size):
    z = 8 if utt_size % 8 == 0 else utt_size
    xh = 2 if (utt_size // z) % 2 == 0 else 1
    return {"xl": seg_size // 2, "core": 2, "y": utt_size // (z * xh), "xh": xh, "z": z}


def shifted(value, axis, by):
    length = 1
    for name in axis:
        length *= lax.axis_size(name)
    pairs = [(i, i + by) for i in range(length) if 0 <= i + by < length]
    return lax.ppermute(value, axis, pairs)


def reverse_bits(value, size):
    result = 0
    bit = 1
    while bit < size:
        result = result * 2 + (value // bit) % 2
        bit *= 2
    return result


def exchange_scatter(slab, axis, dim):
    size = slab.shape[dim]
    index = reverse_bits(lax.axis_index(axis), size)
    bit = size // 2
    while bit >= 1:
        shape = slab.shape
        split = shape[:dim] + (2, shape[dim] // 2) + shape[dim + 1 :]
        halves = slab.reshape(split)
        side = (index // bit) % 2
        mine = lax.dynamic_index_in_dim(halves, side, dim, keepdims=False)
        other = lax.dynamic_index_in_dim(halves, 1 - side, dim, keepdims=False)
        flip = reverse_bits(bit, size)
        pairs = [(i, i ^ flip) for i in range(size)]
        slab = mine + lax.ppermute(other, axis, pairs)
        bit //= 2
    return slab


def round_up(value, step):
    return -(-value // step) * step


def layer_math(delayed, current, conv_one, res_one):
    channels = current.shape[1]
    paired = jnp.concatenate([delayed, current], 1)
    preact = jnp.dot(paired, conv_one, preferred_element_type=jnp.float32)
    gate_width = preact.shape[1] // 2
    gated = (jnp.tanh(preact[:, :gate_width]) * jax.nn.sigmoid(preact[:, gate_width:])).astype(
        jnp.bfloat16
    )
    following = None
    if res_one is not None:
        residual_term = jnp.dot(gated, res_one, preferred_element_type=jnp.float32)
        following = ((current.astype(jnp.float32) + residual_term) * HALF_ROOT).astype(
            jnp.bfloat16
        )
    return gated, following


def per_device(
    audio_waves, lengths, target_ids, input_weight, conv_weight, res_weight, skip_weight
):
    batch_rows, seg_len = audio_waves.shape
    layer_total = conv_weight.shape[0]
    reach = 2**layer_total - 1
    earlier = shifted(audio_waves, SEG, 1)
    window = round_up(seg_len + reach, 16)
    extended = jnp.concatenate([earlier, audio_waves], 1)[0, 2 * seg_len - window :]
    hidden = (extended[:, None] * input_weight[None, :]).astype(jnp.bfloat16)
    gated_list = []
    for layer_num in range(layer_total):
        dilation = 2**layer_num
        later_reach = 2**layer_total - 2 ** (layer_num + 1)
        in_len = hidden.shape[0]
        out_len = min(in_len, round_up(seg_len + later_reach, 16))
        if in_len - dilation >= out_len:
            delayed = hidden[in_len - out_len - dilation : in_len - dilation]
        else:
            delayed = jnp.concatenate(
                [jnp.zeros((dilation, hidden.shape[1]), hidden.dtype), hidden[: in_len - dilation]],
                0,
            )
        current = hidden[in_len - out_len :]
        res_one = res_weight[layer_num] if layer_num < layer_total - 1 else None
        gated, hidden = layer_math(delayed, current, conv_weight[layer_num], res_one)
        gated_list.append(gated[out_len - seg_len :])
    stacked = jnp.concatenate(gated_list, 1)
    skip_sum = jnp.dot(stacked, skip_weight, preferred_element_type=jnp.float32)
    features = jnp.maximum(skip_sum, 0.0).astype(jnp.bfloat16)
    skip_width = features.shape[1]
    position = lax.axis_index(SEG) * seg_len + jnp.arange(seg_len, dtype=jnp.int32)
    valid = (position[None, :] < lengths[:, None]).reshape(batch_rows * seg_len)
    masked = jnp.where(valid[:, None], features, jnp.zeros_like(features))
    frame_ids = jnp.repeat(target_ids, FRAME, axis=1).reshape(batch_rows * seg_len)
    onehot = (frame_ids[:, None] == jnp.arange(CLASSES, dtype=jnp.int32)[None, :]).astype(
        jnp.bfloat16
    )
    paired = jnp.concatenate([masked, onehot], 1)
    sizes = {name: lax.axis_size(name) for name in FINE}
    owners = 1
    for name in FINE:
        owners *= sizes[name]
    row_count = skip_width // owners
    width = paired.shape[1]
    group_sizes = []
    for group in GROUPS:
        size = 1
        for name in group:
            size *= sizes[name]
        group_sizes.append(size)
    pair = group_sizes[-1] * row_count
    local_count = jnp.sum(valid.astype(jnp.float32))
    cores = group_sizes[0]
    core_rows = skip_width // cores
    core = lax.axis_index("core")

    def core_half(part):
        lhs = lax.dynamic_slice_in_dim(masked, part * core_rows, core_rows, 1)
        rows_part = lax.dot_general(
            lhs, paired, (((0,), (0,)), ((), ())), preferred_element_type=jnp.float32
        )
        rows = lax.broadcasted_iota(jnp.int32, rows_part.shape, 0) + part * core_rows
        cols = lax.broadcasted_iota(jnp.int32, rows_part.shape, 1)
        slot = (rows % row_count == 1) & (cols == rows - 1)
        rows_part = jnp.where(slot, local_count, rows_part)
        return rows_part.reshape((1,) + tuple(group_sizes[1:-1]) + (pair, width))

    sent = lax.ppermute(core_half(1 - core), "core", [(i, i ^ 1) for i in range(cores)])
    slab = core_half(core) + sent
    half = width - (width // 128 * 2 // 5) * 128
    left = exchange_scatter(slab[..., :half], "z", 1)
    right = exchange_scatter(slab[..., half:], "y", 2)
    left = exchange_scatter(left, "y", 2)
    right = exchange_scatter(right, "z", 1)
    slab = jnp.concatenate([left, right], -1)
    slab = exchange_scatter(slab, "xh", 3)
    slab = slab.reshape(tuple(slab.shape[:-2]) + (group_sizes[-1], row_count, width))
    slab = exchange_scatter(slab, "xl", 4)
    slab = lax.ppermute(slab, FINE, owner_pairs(sizes))
    owned_rows = slab.reshape(row_count, width)
    first_col = lax.axis_index(FINE) * row_count
    valid_total = lax.dynamic_slice(owned_rows, (1, first_col), (1, 1))[0, 0]
    mirror = lax.dynamic_slice(owned_rows, (0, first_col + 1), (1, 1))[0, 0]
    own_rows = lax.broadcasted_iota(jnp.int32, owned_rows.shape, 0)
    own_cols = lax.broadcasted_iota(jnp.int32, owned_rows.shape, 1)
    owned_rows = jnp.where((own_rows == 1) & (own_cols == first_col), mirror, owned_rows)
    gram_rows = owned_rows[:, :skip_width] / valid_total
    cross_rows = owned_rows[:, skip_width:] * (CLASSES / valid_total)
    return (gram_rows, cross_rows)


def solution(mesh):
    sizes = fine_sizes(mesh.shape["seg"], mesh.shape["utt"])
    fine = Mesh(mesh.devices.reshape(tuple(sizes[n] for n in FINE)), FINE)
    in_specs = (P(UTT, SEG), P(UTT), P(UTT, SEG), P(), P(), P(), P())
    out_specs = (P(FINE, None), P(FINE, None))
    return jax.shard_map(
        per_device, mesh=fine, in_specs=in_specs, out_specs=out_specs, check_vma=False
    )
```
